512 devices in a mesh: dp: 16 (over y, core), comp: 32 (over z, x).
Axes of the slice: x: 4, y: 8, z: 8, core: 2. Of those that a mesh axis runs over, the one named last changes fastest.
Arguments:
- descriptors: bfloat16 [65536, 256], P('dp'), may hold values from -12 to 12
- means: float32 [16384, 256], P('comp'), may hold values from -3 to 3
- variances: float32 [16384, 256], P('comp'), may hold values from 0.5 to 2
- log_weights: float32 [16384], P('comp'), may hold values from -2 to 2
Outputs:
- new_log_weights: float32 [16384], P('comp')
- new_means: float32 [16384, 256], P('comp')
- new_variances: float32 [16384, 256], P('comp')
The draws below stay inside these ranges and needn't reach their ends.
All inputs are finite; a program needn't handle non-finite values.
Results may differ from the reference program's by a relative error of at most 0.002.
Values sent between devices are 32-bit elements; how exact they have to be, the bound alone decides.
No kernel may reach another device: no remote copies, remote signals or barrier semaphores. Data moves between devices by JAX's collectives and lax.ppermute only.
A program may use at most 64 MiB of HBM per device.

```python
import math
import jax
import jax.numpy as jnp
from jax import lax

D = 256
K = 16384
ROWS = 65536


def draw_descriptors(key, part):
    key_core, key_rows, key_cols = jax.random.split(key, 3)
    core = jnp.clip(jax.random.normal(key_core, (ROWS, D), jnp.float32), -4.0, 4.0)
    row_scale = jnp.exp(jax.random.uniform(key_rows, (ROWS, 1), jnp.float32, math.log(0.4), math.log(2.0)))
    col_scale = jnp.exp(jax.random.uniform(key_cols, (1, D), jnp.float32, math.log(0.7), math.log(1.4)))
    return (core * row_scale * col_scale).astype(jnp.bfloat16)


def shard_levels(own_key, shape, shards, least, top_value):
    def one(position, blocks):
        draws = jax.random.uniform(jax.random.fold_in(jax.random.fold_in(own_key, 6), position), (blocks,), jnp.float32, least / len(shards), top_value / len(shards))
        return jnp.repeat(jnp.exp(draws), shape[position] // blocks).reshape((-1,) + (1,) * (len(shape) - position - 1))

    factor_of = one(*shards[0])
    for cut in shards[1:]:
        factor_of = factor_of * one(*cut)
    return factor_of


def normal_values(stream_key, extent, width, reach, cuts=(), held_as=jnp.bfloat16):
    drawn = width * jax.random.normal(stream_key, extent, jnp.float32)
    if cuts:
        drawn = drawn * shard_levels(stream_key, extent, cuts, -0.22, 0.18)
    return jnp.clip(drawn, -reach, reach).astype(held_as)


def setup_inputs(seed: int = 0) -> dict:
    splits = jax.random.split(jax.random.key(seed), 5)
    return {
        "descriptors": draw_descriptors(jax.random.fold_in(splits[4], 71), 0),
        "means": normal_values(splits[1], (K, D), 0.5, 3.0, ((0, 32),), jnp.float32),
        "variances": jnp.clip(jnp.exp(math.log(2.0) - 1.3862944 * jax.random.uniform(splits[2], (K, D), jnp.float32) ** shard_levels(splits[2], (K, D), ((0, 32),), -0.2, 0.2)), 0.5, 2.0),
        "log_weights": jnp.clip(jax.random.uniform(splits[3], (K,), jnp.float32, -2.0, 2.0) * shard_levels(splits[3], (K,), ((0, 32),), -0.4, 0.0), -2.0, 2.0),
    }


prior_count = 1.0
log_two_pi = 1.8378770664093453


def reference(descriptors, means, variances, log_weights):
    row_count = descriptors.shape[0]
    feature_width = descriptors.shape[1]
    components = means.shape[0]
    precision = 1.0 / variances
    scaled_means = means * precision
    loading = jnp.concatenate([-0.5 * precision, scaled_means], axis=1)
    offset = log_weights - 0.5 * jnp.sum(means * scaled_means + jnp.log(variances) + log_two_pi, axis=1)
    block_rows = min(1024, row_count)
    stacked = descriptors.reshape(row_count // block_rows, block_rows, feature_width)

    def accumulate(totals, row_block):
        moments, counts = totals
        exact = row_block.astype(jnp.float32)
        features = jnp.concatenate([exact * exact, exact], axis=1)
        scores = lax.dot_general(features, loading, (((1,), (1,)), ((), ())), precision=lax.Precision.HIGHEST, preferred_element_type=jnp.float32) + offset[None, :]
        highest = jnp.max(scores, axis=1, keepdims=True)
        log_total = highest + jnp.log(jnp.sum(jnp.exp(scores - highest), axis=1, keepdims=True))
        responsibility = jnp.exp(scores - log_total)
        resp_half = responsibility.astype(jnp.bfloat16)
        halves = jnp.concatenate([row_block, (exact * exact).astype(jnp.bfloat16)], axis=1)
        moments = moments + lax.dot_general(resp_half, halves, (((0,), (0,)), ((), ())), preferred_element_type=jnp.float32)
        counts = counts + jnp.sum(responsibility, axis=0)
        return (moments, counts), None

    zeros_pair = (jnp.zeros((components, 2 * feature_width), jnp.float32), jnp.zeros((components,), jnp.float32))
    (moments, counts), _ = lax.scan(accumulate, zeros_pair, stacked)
    weight = counts + prior_count
    new_means = (moments[:, :feature_width] + prior_count * means) / weight[:, None]
    new_variances = (moments[:, feature_width:] + prior_count * (variances + means * means)) / weight[:, None] - new_means * new_means
    new_log_weights = jnp.log(weight) - jnp.log(row_count + prior_count * components)
    return new_log_weights, new_means, new_variances
```

```python
import jax
import jax.numpy as jnp
from jax import lax
from jax.sharding import PartitionSpec as P

prior_count = 1.0
log_two_pi = 1.8378770664093453


def finish(moments, counts, means, variances, grand_total):
    feature_width = means.shape[1]
    weight = counts + prior_count
    new_means = (moments[:, :feature_width] + prior_count * means) / weight[:, None]
    new_variances = (
        moments[:, feature_width:] + prior_count * (variances + means * means)
    ) / weight[:, None] - new_means * new_means
    new_log_weights = jnp.log(weight) - jnp.log(grand_total)
    return (new_log_weights, new_means, new_variances)


def on_device(descriptors, means, variances, log_weights):
    row_count = descriptors.shape[0]
    feature_width = descriptors.shape[1]
    owned_count = means.shape[0]
    grand_total = row_count * lax.axis_size("dp") + prior_count * owned_count * lax.axis_size(
        "comp"
    )
    precision = 1.0 / variances
    scaled_means = means * precision
    loading = jnp.concatenate([-0.5 * precision, scaled_means], axis=1)
    offset = log_weights - 0.5 * jnp.sum(
        means * scaled_means + jnp.log(variances) + log_two_pi, axis=1
    )
    block_rows = min(512, row_count)
    stacked = descriptors.reshape(row_count // block_rows, block_rows, feature_width)

    def score_block(row_block):
        exact = row_block.astype(jnp.float32)
        features = jnp.concatenate([exact * exact, exact], axis=1)
        return (
            lax.dot_general(
                features,
                loading,
                (((1,), (1,)), ((), ())),
                precision=lax.Precision.HIGHEST,
                preferred_element_type=jnp.float32,
            )
            + offset[None, :]
        )

    scores = lax.map(score_block, stacked).reshape(row_count, owned_count)
    local_max = jnp.max(scores, axis=1)
    local_sum = jnp.sum(jnp.exp(scores - local_max[:, None]), axis=1)
    gathered = lax.all_gather(jnp.stack([local_max, local_sum]), "comp")
    row_max = jnp.max(gathered[:, 0], axis=0)
    row_sum = jnp.sum(gathered[:, 1] * jnp.exp(gathered[:, 0] - row_max[None, :]), axis=0)
    log_total = row_max + jnp.log(row_sum)
    responsibility = jnp.exp(scores - log_total[:, None])
    counts = jnp.sum(responsibility, axis=0)
    resp_half = responsibility.astype(jnp.bfloat16)
    exact_rows = descriptors.astype(jnp.float32)
    halves = jnp.concatenate([descriptors, (exact_rows * exact_rows).astype(jnp.bfloat16)], axis=1)
    moments = lax.dot_general(
        resp_half, halves, (((0,), (0,)), ((), ())), preferred_element_type=jnp.float32
    )
    packed = lax.psum(jnp.concatenate([moments, counts[None, :]], axis=0), "dp")
    summed_moments = packed[:owned_count]
    summed_counts = packed[owned_count]
    new_log_weights, new_means, new_variances = finish(
        summed_moments, summed_counts, means, variances, grand_total
    )
    return (new_log_weights, new_means, new_variances)


def solution(mesh):
    placed = (P("dp", None), P("comp", None), P("comp", None), P("comp"))
    return jax.shard_map(
        on_device,
        mesh=mesh,
        in_specs=placed,
        out_specs=(P("comp"), P("comp", None), P("comp", None)),
        check_vma=False,
    )
```

```python
import jax
import jax.numpy as jnp
from jax import lax
from jax.sharding import PartitionSpec as P

prior_count = 1.0
log_two_pi = 1.8378770664093453


def finish(moments, counts, means, variances, grand_total):
    feature_width = means.shape[1]
    weight = counts + prior_count
    new_means = (moments[:, :feature_width] + prior_count * means) / weight[:, None]
    new_variances = (
        moments[:, feature_width:] + prior_count * (variances + means * means)
    ) / weight[:, None] - new_means * new_means
    new_log_weights = jnp.log(weight) - jnp.log(grand_total)
    return (new_log_weights, new_means, new_variances)


def xor_pairs(size, bit):
    return [(i, i ^ bit) for i in range(size)]


def row_logsumexp_stats(local_max, local_sum, axis):
    size = lax.axis_size(axis)
    row_max, row_sum = local_max, local_sum
    bit = 1
    while bit < size:
        other = lax.ppermute(jnp.stack([row_max, row_sum]), axis, xor_pairs(size, bit))
        other_max, other_sum = other[0], other[1]
        new_max = jnp.maximum(row_max, other_max)
        row_sum = row_sum * jnp.exp(row_max - new_max) + other_sum * jnp.exp(other_max - new_max)
        row_max = new_max
        bit *= 2
    return row_max, row_sum


def halving_psum(rows, axis):
    size = lax.axis_size(axis)
    index = lax.axis_index(axis)
    current = rows
    bits = []
    bit = 1
    while bit < size:
        half = current.shape[0] // 2
        low, high = current[:half], current[half:]
        upper = (index // bit) % 2 == 1
        keep = jnp.where(upper, high, low)
        send = jnp.where(upper, low, high)
        current = keep + lax.ppermute(send, axis, xor_pairs(size, bit))
        bits.append(bit)
        bit *= 2
    for bit in reversed(bits):
        upper = (index // bit) % 2 == 1
        other = lax.ppermute(current, axis, xor_pairs(size, bit))
        current = jnp.where(
            upper, jnp.concatenate([other, current]), jnp.concatenate([current, other])
        )
    return current


def on_device(descriptors, means, variances, log_weights):
    row_count = descriptors.shape[0]
    feature_width = descriptors.shape[1]
    owned_count = means.shape[0]
    grand_total = row_count * lax.axis_size("dp") + prior_count * owned_count * lax.axis_size(
        "comp"
    )
    precision = 1.0 / variances
    scaled_means = means * precision
    loading = jnp.concatenate([-0.5 * precision, scaled_means], axis=1)
    offset = log_weights - 0.5 * jnp.sum(
        means * scaled_means + jnp.log(variances) + log_two_pi, axis=1
    )
    block_rows = min(512, row_count)
    stacked = descriptors.reshape(row_count // block_rows, block_rows, feature_width)

    def score_block(row_block):
        exact = row_block.astype(jnp.float32)
        features = jnp.concatenate([exact * exact, exact], axis=1)
        return (
            lax.dot_general(
                features,
                loading,
                (((1,), (1,)), ((), ())),
                precision=lax.Precision.HIGHEST,
                preferred_element_type=jnp.float32,
            )
            + offset[None, :]
        )

    scores = lax.map(score_block, stacked).reshape(row_count, owned_count)
    local_max = jnp.max(scores, axis=1)
    local_sum = jnp.sum(jnp.exp(scores - local_max[:, None]), axis=1)
    row_max, row_sum = row_logsumexp_stats(local_max, local_sum, "comp")
    log_total = row_max + jnp.log(row_sum)
    responsibility = jnp.exp(scores - log_total[:, None])
    counts = jnp.sum(responsibility, axis=0)
    resp_half = responsibility.astype(jnp.bfloat16)
    exact_rows = descriptors.astype(jnp.float32)
    halves = jnp.concatenate([descriptors, (exact_rows * exact_rows).astype(jnp.bfloat16)], axis=1)
    moments = lax.dot_general(
        resp_half, halves, (((0,), (0,)), ((), ())), preferred_element_type=jnp.float32
    )
    lanes = 128
    dp_size = lax.axis_size("dp")
    flat_rows = (moments.size + counts.size) // lanes
    unit = 8 * dp_size
    padded_rows = -(-flat_rows // unit) * unit
    packed = jnp.concatenate(
        [
            moments.reshape(-1, lanes),
            counts.reshape(-1, lanes),
            jnp.zeros((padded_rows - flat_rows, lanes), jnp.float32),
        ]
    )
    summed = halving_psum(packed, "dp")
    moment_rows = moments.size // lanes
    summed_moments = summed[:moment_rows].reshape(moments.shape)
    summed_counts = summed[moment_rows:flat_rows].reshape(counts.shape)
    new_log_weights, new_means, new_variances = finish(
        summed_moments, summed_counts, means, variances, grand_total
    )
    return (new_log_weights, new_means, new_variances)


def solution(mesh):
    placed = (P("dp", None), P("comp", None), P("comp", None), P("comp"))
    return jax.shard_map(
        on_device,
        mesh=mesh,
        in_specs=placed,
        out_specs=(P("comp"), P("comp", None), P("comp", None)),
        check_vma=False,
    )
```

```python
import jax
import jax.numpy as jnp
from jax import lax
from jax.sharding import PartitionSpec as P


prior_count = 1.0
log_two_pi = 1.8378770664093453


def finish(moments, counts, means, variances, grand_total):
    feature_width = means.shape[1]
    weight = counts + prior_count
    new_means = (moments[:, :feature_width] + prior_count * means) / weight[:, None]
    new_variances = (
        moments[:, feature_width:] + prior_count * (variances + means * means)
    ) / weight[:, None] - new_means * new_means
    new_log_weights = jnp.log(weight) - jnp.log(grand_total)
    return (new_log_weights, new_means, new_variances)


def xor_pairs(size, bit):
    return [(i, i ^ bit) for i in range(size)]


def row_logsumexp_stats(local_max, local_sum, axis):
    size = lax.axis_size(axis)
    row_max, row_sum = local_max, local_sum
    bit = 1
    while bit < size:
        other = lax.ppermute(jnp.stack([row_max, row_sum]), axis, xor_pairs(size, bit))
        other_max, other_sum = other[0], other[1]
        new_max = jnp.maximum(row_max, other_max)
        row_sum = row_sum * jnp.exp(row_max - new_max) + other_sum * jnp.exp(other_max - new_max)
        row_max = new_max
        bit *= 2
    return row_max, row_sum


def chip_direct_psum(rows, axis):
    size = lax.axis_size(axis)
    index = lax.axis_index(axis)
    chips = size // 2
    chip = index // 2
    upper = index % 2 == 1
    half = rows.shape[0] // 2
    low, high = rows[:half], rows[half:]
    mine = jnp.where(upper, high, low) + lax.ppermute(
        jnp.where(upper, low, high), axis, xor_pairs(size, 1)
    )
    pieces = mine.reshape(chips, half // chips, mine.shape[1])
    total = lax.dynamic_index_in_dim(pieces, chip, 0, keepdims=False)
    for step in range(1, chips):
        outgoing = lax.dynamic_index_in_dim(pieces, chip ^ step, 0, keepdims=False)
        total = total + lax.ppermute(outgoing, axis, xor_pairs(size, 2 * step))
    arrived = [total] + [
        lax.ppermute(total, axis, xor_pairs(size, 2 * step)) for step in range(1, chips)
    ]
    order = jnp.arange(chips) ^ chip
    gathered = jnp.stack(arrived)[order].reshape(half, mine.shape[1])
    other = lax.ppermute(gathered, axis, xor_pairs(size, 1))
    return jnp.where(
        upper, jnp.concatenate([other, gathered]), jnp.concatenate([gathered, other])
    )


def on_device(descriptors, means, variances, log_weights):
    row_count = descriptors.shape[0]
    feature_width = descriptors.shape[1]
    owned_count = means.shape[0]
    grand_total = row_count * lax.axis_size("dp") + prior_count * owned_count * lax.axis_size(
        "comp"
    )
    precision = 1.0 / variances
    scaled_means = means * precision
    loading = jnp.concatenate([-0.5 * precision, scaled_means], axis=1)
    offset = log_weights - 0.5 * jnp.sum(
        means * scaled_means + jnp.log(variances) + log_two_pi, axis=1
    )
    block_rows = min(512, row_count)
    stacked = descriptors.reshape(row_count // block_rows, block_rows, feature_width)

    def score_block(row_block):
        exact = row_block.astype(jnp.float32)
        features = jnp.concatenate([exact * exact, exact], axis=1)
        return (
            lax.dot_general(
                features,
                loading,
                (((1,), (1,)), ((), ())),
                precision=lax.Precision.HIGHEST,
                preferred_element_type=jnp.float32,
            )
            + offset[None, :]
        )

    scores = lax.map(score_block, stacked).reshape(row_count, owned_count)
    local_max = jnp.max(scores, axis=1)
    local_sum = jnp.sum(jnp.exp(scores - local_max[:, None]), axis=1)
    row_max, row_sum = row_logsumexp_stats(local_max, local_sum, "comp")
    log_total = row_max + jnp.log(row_sum)
    responsibility = jnp.exp(scores - log_total[:, None])
    counts = jnp.sum(responsibility, axis=0)
    resp_half = responsibility.astype(jnp.bfloat16)
    exact_rows = descriptors.astype(jnp.float32)
    halves = jnp.concatenate([descriptors, (exact_rows * exact_rows).astype(jnp.bfloat16)], axis=1)
    moments = lax.dot_general(
        resp_half, halves, (((0,), (0,)), ((), ())), preferred_element_type=jnp.float32
    )
    lanes = 128
    dp_size = lax.axis_size("dp")
    flat_rows = (moments.size + counts.size) // lanes
    unit = 8 * dp_size
    padded_rows = -(-flat_rows // unit) * unit
    packed = jnp.concatenate(
        [
            moments.reshape(-1, lanes),
            counts.reshape(-1, lanes),
            jnp.zeros((padded_rows - flat_rows, lanes), jnp.float32),
        ]
    )
    summed = chip_direct_psum(packed, "dp")
    moment_rows = moments.size // lanes
    summed_moments = summed[:moment_rows].reshape(moments.shape)
    summed_counts = summed[moment_rows:flat_rows].reshape(counts.shape)
    new_log_weights, new_means, new_variances = finish(
        summed_moments, summed_counts, means, variances, grand_total
    )
    return (new_log_weights, new_means, new_variances)


def solution(mesh):
    placed = (P("dp", None), P("comp", None), P("comp", None), P("comp"))
    return jax.shard_map(
        on_device,
        mesh=mesh,
        in_specs=placed,
        out_specs=(P("comp"), P("comp", None), P("comp", None)),
        check_vma=False,
    )
```

```python
import jax
import jax.numpy as jnp
from jax import lax
from jax.sharding import PartitionSpec as P


prior_count = 1.0
log_two_pi = 1.8378770664093453


def finish(moments, counts, means, variances, grand_total):
    feature_width = means.shape[1]
    weight = counts + prior_count
    new_means = (moments[:, :feature_width] + prior_count * means) / weight[:, None]
    new_variances = (
        moments[:, feature_width:] + prior_count * (variances + means * means)
    ) / weight[:, None] - new_means * new_means
    new_log_weights = jnp.log(weight) - jnp.log(grand_total)
    return (new_log_weights, new_means, new_variances)


def xor_pairs(size, bit):
    return [(i, i ^ bit) for i in range(size)]


def row_logsumexp_stats(local_max, local_sum, axis):
    size = lax.axis_size(axis)
    row_max, row_sum = local_max, local_sum
    bit = 1
    while bit < size:
        other = lax.ppermute(jnp.stack([row_max, row_sum]), axis, xor_pairs(size, bit))
        other_max, other_sum = other[0], other[1]
        new_max = jnp.maximum(row_max, other_max)
        row_sum = row_sum * jnp.exp(row_max - new_max) + other_sum * jnp.exp(other_max - new_max)
        row_max = new_max
        bit *= 2
    return row_max, row_sum


def chip_doubling_psum(rows, axis):
    size = lax.axis_size(axis)
    index = lax.axis_index(axis)
    upper = index % 2 == 1
    half = rows.shape[0] // 2
    low, high = rows[:half], rows[half:]
    mine = jnp.where(upper, high, low) + lax.ppermute(
        jnp.where(upper, low, high), axis, xor_pairs(size, 1)
    )
    bit = 2
    while bit < size:
        mine = mine + lax.ppermute(mine, axis, xor_pairs(size, bit))
        bit *= 2
    other = lax.ppermute(mine, axis, xor_pairs(size, 1))
    return jnp.where(upper, jnp.concatenate([other, mine]), jnp.concatenate([mine, other]))


def on_device(descriptors, means, variances, log_weights):
    row_count = descriptors.shape[0]
    feature_width = descriptors.shape[1]
    owned_count = means.shape[0]
    grand_total = row_count * lax.axis_size("dp") + prior_count * owned_count * lax.axis_size(
        "comp"
    )
    precision = 1.0 / variances
    scaled_means = means * precision
    loading = jnp.concatenate([-0.5 * precision, scaled_means], axis=1)
    offset = log_weights - 0.5 * jnp.sum(
        means * scaled_means + jnp.log(variances) + log_two_pi, axis=1
    )
    block_rows = min(512, row_count)
    stacked = descriptors.reshape(row_count // block_rows, block_rows, feature_width)

    def score_block(row_block):
        exact = row_block.astype(jnp.float32)
        features = jnp.concatenate([exact * exact, exact], axis=1)
        return (
            lax.dot_general(
                features,
                loading,
                (((1,), (1,)), ((), ())),
                precision=lax.Precision.HIGHEST,
                preferred_element_type=jnp.float32,
            )
            + offset[None, :]
        )

    scores = lax.map(score_block, stacked).reshape(row_count, owned_count)
    local_max = jnp.max(scores, axis=1)
    local_sum = jnp.sum(jnp.exp(scores - local_max[:, None]), axis=1)
    row_max, row_sum = row_logsumexp_stats(local_max, local_sum, "comp")
    log_total = row_max + jnp.log(row_sum)
    responsibility = jnp.exp(scores - log_total[:, None])
    counts = jnp.sum(responsibility, axis=0)
    resp_half = responsibility.astype(jnp.bfloat16)
    exact_rows = descriptors.astype(jnp.float32)
    halves = jnp.concatenate([descriptors, (exact_rows * exact_rows).astype(jnp.bfloat16)], axis=1)
    moments = lax.dot_general(
        resp_half, halves, (((0,), (0,)), ((), ())), preferred_element_type=jnp.float32
    )
    lanes = 128
    flat_rows = (moments.size + counts.size) // lanes
    unit = 16
    padded_rows = -(-flat_rows // unit) * unit
    packed = jnp.concatenate(
        [
            moments.reshape(-1, lanes),
            counts.reshape(-1, lanes),
            jnp.zeros((padded_rows - flat_rows, lanes), jnp.float32),
        ]
    )
    summed = chip_doubling_psum(packed, "dp")
    moment_rows = moments.size // lanes
    summed_moments = summed[:moment_rows].reshape(moments.shape)
    summed_counts = summed[moment_rows:flat_rows].reshape(counts.shape)
    new_log_weights, new_means, new_variances = finish(
        summed_moments, summed_counts, means, variances, grand_total
    )
    return (new_log_weights, new_means, new_variances)


def solution(mesh):
    placed = (P("dp", None), P("comp", None), P("comp", None), P("comp"))
    return jax.shard_map(
        on_device,
        mesh=mesh,
        in_specs=placed,
        out_specs=(P("comp"), P("comp", None), P("comp", None)),
        check_vma=False,
    )
```

```python
import jax
import jax.numpy as jnp
from jax import lax
from jax.sharding import PartitionSpec as P


prior_count = 1.0
log_two_pi = 1.8378770664093453


def finish(moments, counts, means, variances, grand_total):
    feature_width = means.shape[1]
    weight = counts + prior_count
    new_means = (moments[:, :feature_width] + prior_count * means) / weight[:, None]
    new_variances = (
        moments[:, feature_width:] + prior_count * (variances + means * means)
    ) / weight[:, None] - new_means * new_means
    new_log_weights = jnp.log(weight) - jnp.log(grand_total)
    return (new_log_weights, new_means, new_variances)


def xor_pairs(size, bit):
    return [(i, i ^ bit) for i in range(size)]


def row_logsumexp_stats(local_max, local_sum, axis):
    size = lax.axis_size(axis)
    row_max, row_sum = local_max, local_sum
    bit = 1
    while bit < size:
        other = lax.ppermute(jnp.stack([row_max, row_sum]), axis, xor_pairs(size, bit))
        other_max, other_sum = other[0], other[1]
        new_max = jnp.maximum(row_max, other_max)
        row_sum = row_sum * jnp.exp(row_max - new_max) + other_sum * jnp.exp(other_max - new_max)
        row_max = new_max
        bit *= 2
    return row_max, row_sum


def halving_psum(rows, axis):
    size = lax.axis_size(axis)
    index = lax.axis_index(axis)
    current = rows
    bits = []
    bit = 1
    while bit < size:
        half = current.shape[0] // 2
        low, high = current[:half], current[half:]
        upper = (index // bit) % 2 == 1
        keep = jnp.where(upper, high, low)
        send = jnp.where(upper, low, high)
        current = keep + lax.ppermute(send, axis, xor_pairs(size, bit))
        bits.append(bit)
        bit *= 2
    for bit in reversed(bits):
        upper = (index // bit) % 2 == 1
        other = lax.ppermute(current, axis, xor_pairs(size, bit))
        current = jnp.where(
            upper, jnp.concatenate([other, current]), jnp.concatenate([current, other])
        )
    return current


def on_device(descriptors, means, variances, log_weights):
    row_count = descriptors.shape[0]
    feature_width = descriptors.shape[1]
    owned_count = means.shape[0]
    grand_total = row_count * lax.axis_size("dp") + prior_count * owned_count * lax.axis_size(
        "comp"
    )
    precision = 1.0 / variances
    scaled_means = means * precision
    offset = log_weights - 0.5 * jnp.sum(
        means * scaled_means + jnp.log(variances) + log_two_pi, axis=1
    )

    def rounded(values):
        return lax.reduce_precision(values, exponent_bits=8, mantissa_bits=7)

    def pieces(values):
        first = rounded(values)
        rest = values - first
        second = rounded(rest)
        third = rounded(rest - second)
        return (
            first.astype(jnp.bfloat16),
            second.astype(jnp.bfloat16),
            third.astype(jnp.bfloat16),
        )

    p1, p2, p3 = pieces(-0.5 * precision)
    m1, m2, m3 = pieces(scaled_means)
    loading_a = jnp.concatenate([p1, p1, m1], axis=1)
    loading_b = jnp.concatenate([p2, p2, m2], axis=1)
    loading_c = jnp.concatenate([p3, m3], axis=1)
    block_rows = min(512, row_count)
    stacked = descriptors.reshape(row_count // block_rows, block_rows, feature_width)

    def score_block(row_block):
        exact = row_block.astype(jnp.float32)
        square = exact * exact
        square_top = rounded(square)
        square_hi = square_top.astype(jnp.bfloat16)
        square_lo = (square - square_top).astype(jnp.bfloat16)
        wide = jnp.concatenate([square_hi, square_lo, row_block], axis=1)
        narrow = jnp.concatenate([square_hi, row_block], axis=1)

        def product(features, loading):
            return lax.dot_general(
                features,
                loading,
                (((1,), (1,)), ((), ())),
                preferred_element_type=jnp.float32,
            )

        return (
            product(wide, loading_a) + product(wide, loading_b) + product(narrow, loading_c)
        ) + offset[None, :]

    scores = lax.map(score_block, stacked).reshape(row_count, owned_count)
    local_max = jnp.max(scores, axis=1)
    local_sum = jnp.sum(jnp.exp(scores - local_max[:, None]), axis=1)
    row_max, row_sum = row_logsumexp_stats(local_max, local_sum, "comp")
    log_total = row_max + jnp.log(row_sum)
    responsibility = jnp.exp(scores - log_total[:, None])
    counts = jnp.sum(responsibility, axis=0)
    resp_half = responsibility.astype(jnp.bfloat16)
    exact_rows = descriptors.astype(jnp.float32)
    halves = jnp.concatenate([descriptors, (exact_rows * exact_rows).astype(jnp.bfloat16)], axis=1)
    moments = lax.dot_general(
        resp_half, halves, (((0,), (0,)), ((), ())), preferred_element_type=jnp.float32
    )
    lanes = 128
    dp_size = lax.axis_size("dp")
    flat_rows = (moments.size + counts.size) // lanes
    unit = 8 * dp_size
    padded_rows = -(-flat_rows // unit) * unit
    packed = jnp.concatenate(
        [
            moments.reshape(-1, lanes),
            counts.reshape(-1, lanes),
            jnp.zeros((padded_rows - flat_rows, lanes), jnp.float32),
        ]
    )
    summed = halving_psum(packed, "dp")
    moment_rows = moments.size // lanes
    summed_moments = summed[:moment_rows].reshape(moments.shape)
    summed_counts = summed[moment_rows:flat_rows].reshape(counts.shape)
    new_log_weights, new_means, new_variances = finish(
        summed_moments, summed_counts, means, variances, grand_total
    )
    return (new_log_weights, new_means, new_variances)


def solution(mesh):
    placed = (P("dp", None), P("comp", None), P("comp", None), P("comp"))
    return jax.shard_map(
        on_device,
        mesh=mesh,
        in_specs=placed,
        out_specs=(P("comp"), P("comp", None), P("comp", None)),
        check_vma=False,
    )
```

```python
import jax
import jax.numpy as jnp
from jax import lax
from jax.sharding import PartitionSpec as P


prior_count = 1.0
log_two_pi = 1.8378770664093453


def finish(moments, counts, means, variances, grand_total):
    feature_width = means.shape[1]
    weight = counts + prior_count
    new_means = (moments[:, :feature_width] + prior_count * means) / weight[:, None]
    new_variances = (
        moments[:, feature_width:] + prior_count * (variances + means * means)
    ) / weight[:, None] - new_means * new_means
    new_log_weights = jnp.log(weight) - jnp.log(grand_total)
    return (new_log_weights, new_means, new_variances)


def xor_pairs(size, bit):
    return [(i, i ^ bit) for i in range(size)]


def row_logsumexp_stats(local_max, local_sum, axis):
    size = lax.axis_size(axis)
    row_max, row_sum = local_max, local_sum
    bit = 1
    while bit < size:
        other = lax.ppermute(jnp.stack([row_max, row_sum]), axis, xor_pairs(size, bit))
        other_max, other_sum = other[0], other[1]
        new_max = jnp.maximum(row_max, other_max)
        row_sum = row_sum * jnp.exp(row_max - new_max) + other_sum * jnp.exp(other_max - new_max)
        row_max = new_max
        bit *= 2
    return row_max, row_sum


def halving_psum(rows, axis):
    size = lax.axis_size(axis)
    index = lax.axis_index(axis)
    current = rows
    bits = []
    bit = 1
    while bit < size:
        half = current.shape[0] // 2
        low, high = current[:half], current[half:]
        upper = (index // bit) % 2 == 1
        keep = jnp.where(upper, high, low)
        send = jnp.where(upper, low, high)
        current = keep + lax.ppermute(send, axis, xor_pairs(size, bit))
        bits.append(bit)
        bit *= 2
    for bit in reversed(bits):
        upper = (index // bit) % 2 == 1
        other = lax.ppermute(current, axis, xor_pairs(size, bit))
        current = jnp.where(
            upper, jnp.concatenate([other, current]), jnp.concatenate([current, other])
        )
    return current


def on_device(descriptors, means, variances, log_weights):
    row_count = descriptors.shape[0]
    feature_width = descriptors.shape[1]
    owned_count = means.shape[0]
    grand_total = row_count * lax.axis_size("dp") + prior_count * owned_count * lax.axis_size(
        "comp"
    )
    precision = 1.0 / variances
    scaled_means = means * precision
    offset = log_weights - 0.5 * jnp.sum(
        means * scaled_means + jnp.log(variances) + log_two_pi, axis=1
    )

    def rounded(values):
        return lax.reduce_precision(values, exponent_bits=8, mantissa_bits=7)

    def pieces(values):
        first = rounded(values)
        rest = values - first
        second = rounded(rest)
        third = rounded(rest - second)
        return (
            first.astype(jnp.bfloat16),
            second.astype(jnp.bfloat16),
            third.astype(jnp.bfloat16),
        )

    p1, p2, p3 = pieces(-0.5 * precision)
    m1, m2, m3 = pieces(scaled_means)
    loading_a = jnp.concatenate([p1, p1, m1], axis=1)
    loading_b = jnp.concatenate([p2, p2, m2], axis=1)
    loading_c = jnp.concatenate([p3, m3], axis=1)

    def score_block(row_block):
        exact = row_block.astype(jnp.float32)
        square = exact * exact
        square_top = rounded(square)
        square_hi = square_top.astype(jnp.bfloat16)
        square_lo = (square - square_top).astype(jnp.bfloat16)
        wide = jnp.concatenate([square_hi, square_lo, row_block], axis=1)
        narrow = jnp.concatenate([square_hi, row_block], axis=1)

        def product(features, loading):
            return lax.dot_general(
                features,
                loading,
                (((1,), (1,)), ((), ())),
                preferred_element_type=jnp.float32,
            )

        return (
            product(wide, loading_a) + product(wide, loading_b) + product(narrow, loading_c)
        ) + offset[None, :]

    scores = score_block(descriptors)
    local_max = jnp.max(scores, axis=1)
    local_sum = jnp.sum(jnp.exp(scores - local_max[:, None]), axis=1)
    row_max, row_sum = row_logsumexp_stats(local_max, local_sum, "comp")
    log_total = row_max + jnp.log(row_sum)
    responsibility = jnp.exp(scores - log_total[:, None])
    counts = jnp.sum(responsibility, axis=0)
    resp_half = responsibility.astype(jnp.bfloat16)
    exact_rows = descriptors.astype(jnp.float32)
    halves = jnp.concatenate([descriptors, (exact_rows * exact_rows).astype(jnp.bfloat16)], axis=1)
    moments = lax.dot_general(
        resp_half, halves, (((0,), (0,)), ((), ())), preferred_element_type=jnp.float32
    )
    lanes = 128
    dp_size = lax.axis_size("dp")
    flat_rows = (moments.size + counts.size) // lanes
    unit = 8 * dp_size
    padded_rows = -(-flat_rows // unit) * unit
    packed = jnp.concatenate(
        [
            moments.reshape(-1, lanes),
            counts.reshape(-1, lanes),
            jnp.zeros((padded_rows - flat_rows, lanes), jnp.float32),
        ]
    )
    summed = halving_psum(packed, "dp")
    moment_rows = moments.size // lanes
    summed_moments = summed[:moment_rows].reshape(moments.shape)
    summed_counts = summed[moment_rows:flat_rows].reshape(counts.shape)
    new_log_weights, new_means, new_variances = finish(
        summed_moments, summed_counts, means, variances, grand_total
    )
    return (new_log_weights, new_means, new_variances)


def solution(mesh):
    placed = (P("dp", None), P("comp", None), P("comp", None), P("comp"))
    return jax.shard_map(
        on_device,
        mesh=mesh,
        in_specs=placed,
        out_specs=(P("comp"), P("comp", None), P("comp", None)),
        check_vma=False,
    )
```

```python
import jax
import jax.numpy as jnp
from jax import lax
from jax.sharding import PartitionSpec as P


prior_count = 1.0
log_two_pi = 1.8378770664093453


def finish(moments, counts, means, variances, grand_total):
    feature_width = means.shape[1]
    weight = counts + prior_count
    new_means = (moments[:, :feature_width] + prior_count * means) / weight[:, None]
    new_variances = (
        moments[:, feature_width:] + prior_count * (variances + means * means)
    ) / weight[:, None] - new_means * new_means
    new_log_weights = jnp.log(weight) - jnp.log(grand_total)
    return (new_log_weights, new_means, new_variances)


def xor_pairs(size, bit):
    return [(i, i ^ bit) for i in range(size)]


def row_logsumexp_stats(local_max, local_sum, axis):
    size = lax.axis_size(axis)
    row_max, row_sum = local_max, local_sum
    bit = 1
    while bit < size:
        other = lax.ppermute(jnp.stack([row_max, row_sum]), axis, xor_pairs(size, bit))
        other_max, other_sum = other[0], other[1]
        new_max = jnp.maximum(row_max, other_max)
        row_sum = row_sum * jnp.exp(row_max - new_max) + other_sum * jnp.exp(other_max - new_max)
        row_max = new_max
        bit *= 2
    return row_max, row_sum


def halving_psum(rows, axis):
    size = lax.axis_size(axis)
    index = lax.axis_index(axis)
    current = rows
    steps = []
    bit = 1
    while bit < size:
        dim = 1 if bit == 1 else 0
        half = current.shape[dim] // 2
        low = lax.slice_in_dim(current, 0, half, axis=dim)
        high = lax.slice_in_dim(current, half, 2 * half, axis=dim)
        upper = (index // bit) % 2 == 1
        keep = jnp.where(upper, high, low)
        send = jnp.where(upper, low, high)
        current = keep + lax.ppermute(send, axis, xor_pairs(size, bit))
        steps.append((bit, dim))
        bit *= 2
    for bit, dim in reversed(steps):
        upper = (index // bit) % 2 == 1
        other = lax.ppermute(current, axis, xor_pairs(size, bit))
        current = jnp.where(
            upper,
            jnp.concatenate([other, current], axis=dim),
            jnp.concatenate([current, other], axis=dim),
        )
    return current


def on_device(descriptors, means, variances, log_weights):
    row_count = descriptors.shape[0]
    feature_width = descriptors.shape[1]
    owned_count = means.shape[0]
    grand_total = row_count * lax.axis_size("dp") + prior_count * owned_count * lax.axis_size(
        "comp"
    )
    precision = 1.0 / variances
    scaled_means = means * precision
    offset = log_weights - 0.5 * jnp.sum(
        means * scaled_means + jnp.log(variances) + log_two_pi, axis=1
    )

    def rounded(values):
        return lax.reduce_precision(values, exponent_bits=8, mantissa_bits=7)

    def pieces(values):
        first = rounded(values)
        rest = values - first
        second = rounded(rest)
        third = rounded(rest - second)
        return (
            first.astype(jnp.bfloat16),
            second.astype(jnp.bfloat16),
            third.astype(jnp.bfloat16),
        )

    p1, p2, p3 = pieces(-0.5 * precision)
    m1, m2, m3 = pieces(scaled_means)
    loading_a = jnp.concatenate([p1, p1, m1], axis=1)
    loading_b = jnp.concatenate([p2, p2, m2], axis=1)
    loading_c = jnp.concatenate([p3, m3], axis=1)

    def score_block(row_block):
        exact = row_block.astype(jnp.float32)
        square = exact * exact
        square_top = rounded(square)
        square_hi = square_top.astype(jnp.bfloat16)
        square_lo = (square - square_top).astype(jnp.bfloat16)
        wide = jnp.concatenate([square_hi, square_lo, row_block], axis=1)
        narrow = jnp.concatenate([square_hi, row_block], axis=1)

        def product(features, loading):
            return lax.dot_general(
                features,
                loading,
                (((1,), (1,)), ((), ())),
                preferred_element_type=jnp.float32,
            )

        return (
            product(wide, loading_a) + product(wide, loading_b) + product(narrow, loading_c)
        ) + offset[None, :]

    scores = score_block(descriptors)
    local_max = jnp.max(scores, axis=1)
    local_sum = jnp.sum(jnp.exp(scores - local_max[:, None]), axis=1)
    row_max, row_sum = row_logsumexp_stats(local_max, local_sum, "comp")
    log_total = row_max + jnp.log(row_sum)
    responsibility = jnp.exp(scores - log_total[:, None])
    counts = jnp.sum(responsibility, axis=0)
    resp_half = responsibility.astype(jnp.bfloat16)
    exact_rows = descriptors.astype(jnp.float32)
    halves = jnp.concatenate([descriptors, (exact_rows * exact_rows).astype(jnp.bfloat16)], axis=1)
    moments = lax.dot_general(
        resp_half, halves, (((0,), (0,)), ((), ())), preferred_element_type=jnp.float32
    )
    unit = 8 * (lax.axis_size("dp") // 2)
    padded_rows = -(-(owned_count + 1) // unit) * unit
    packed = jnp.concatenate(
        [
            moments,
            jnp.pad(counts, (0, moments.shape[1] - owned_count))[None, :],
            jnp.zeros((padded_rows - owned_count - 1, moments.shape[1]), jnp.float32),
        ]
    )
    summed = halving_psum(packed, "dp")
    summed_moments = summed[:owned_count]
    summed_counts = summed[owned_count, :owned_count]
    new_log_weights, new_means, new_variances = finish(
        summed_moments, summed_counts, means, variances, grand_total
    )
    return (new_log_weights, new_means, new_variances)


def solution(mesh):
    placed = (P("dp", None), P("comp", None), P("comp", None), P("comp"))
    return jax.shard_map(
        on_device,
        mesh=mesh,
        in_specs=placed,
        out_specs=(P("comp"), P("comp", None), P("comp", None)),
        check_vma=False,
    )
```

```python
import jax
import jax.numpy as jnp
from jax import lax
from jax.experimental import pallas as pl
from jax.sharding import PartitionSpec as P


prior_count = 1.0
log_two_pi = 1.8378770664093453


def finish(moments, counts, means, variances, grand_total):
    feature_width = means.shape[1]
    weight = counts + prior_count
    new_means = (moments[:, :feature_width] + prior_count * means) / weight[:, None]
    new_variances = (
        moments[:, feature_width:] + prior_count * (variances + means * means)
    ) / weight[:, None] - new_means * new_means
    new_log_weights = jnp.log(weight) - jnp.log(grand_total)
    return (new_log_weights, new_means, new_variances)


def score_kernel(hi_ref, lo_ref, x_ref, loads_ref, offset_ref, scores_ref, max_ref, sum_ref):
    def product(features, piece):
        return jnp.dot(features, loads_ref[piece], preferred_element_type=jnp.float32)

    hi = hi_ref[...]
    lo = lo_ref[...]
    x = x_ref[...]
    total = product(hi, 0) + product(lo, 0) + product(x, 3)
    total = total + (product(hi, 1) + product(lo, 1) + product(x, 4))
    total = total + (product(hi, 2) + product(x, 5))
    scores = total + offset_ref[...]
    scores_ref[...] = scores
    row_max = jnp.max(scores, axis=1, keepdims=True)
    max_ref[...] = row_max
    sum_ref[...] = jnp.sum(jnp.exp(scores - row_max), axis=1, keepdims=True)


def score_stats(square_hi, square_lo, descriptors, loads, offset):
    rows, width = descriptors.shape
    owned = loads.shape[2]
    block = min(512, rows)
    row_spec = pl.BlockSpec((block, width), lambda i: (i, 0))
    column = jax.ShapeDtypeStruct((rows, 1), jnp.float32)
    return pl.pallas_call(
        score_kernel,
        grid=(rows // block,),
        in_specs=[
            row_spec,
            row_spec,
            row_spec,
            pl.BlockSpec(loads.shape, lambda i: (0, 0, 0)),
            pl.BlockSpec((1, owned), lambda i: (0, 0)),
        ],
        out_specs=[
            pl.BlockSpec((block, owned), lambda i: (i, 0)),
            pl.BlockSpec((block, 1), lambda i: (i, 0)),
            pl.BlockSpec((block, 1), lambda i: (i, 0)),
        ],
        out_shape=[jax.ShapeDtypeStruct((rows, owned), jnp.float32), column, column],
    )(square_hi, square_lo, descriptors, loads, offset[None, :])


def xor_pairs(size, bit):
    return [(i, i ^ bit) for i in range(size)]


def row_logsumexp_stats(local_max, local_sum, axis):
    size = lax.axis_size(axis)
    row_max, row_sum = local_max, local_sum
    bit = 1
    while bit < size:
        other = lax.ppermute(jnp.stack([row_max, row_sum]), axis, xor_pairs(size, bit))
        other_max, other_sum = other[0], other[1]
        new_max = jnp.maximum(row_max, other_max)
        row_sum = row_sum * jnp.exp(row_max - new_max) + other_sum * jnp.exp(other_max - new_max)
        row_max = new_max
        bit *= 2
    return row_max, row_sum


def halving_psum(rows, axis):
    size = lax.axis_size(axis)
    index = lax.axis_index(axis)
    current = rows
    steps = []
    bit = 1
    while bit < size:
        dim = 1 if bit == 1 else 0
        half = current.shape[dim] // 2
        low = lax.slice_in_dim(current, 0, half, axis=dim)
        high = lax.slice_in_dim(current, half, 2 * half, axis=dim)
        upper = (index // bit) % 2 == 1
        keep = jnp.where(upper, high, low)
        send = jnp.where(upper, low, high)
        current = keep + lax.ppermute(send, axis, xor_pairs(size, bit))
        steps.append((bit, dim))
        bit *= 2
    for bit, dim in reversed(steps):
        upper = (index // bit) % 2 == 1
        other = lax.ppermute(current, axis, xor_pairs(size, bit))
        current = jnp.where(
            upper,
            jnp.concatenate([other, current], axis=dim),
            jnp.concatenate([current, other], axis=dim),
        )
    return current


def on_device(descriptors, means, variances, log_weights):
    row_count = descriptors.shape[0]
    feature_width = descriptors.shape[1]
    owned_count = means.shape[0]
    grand_total = row_count * lax.axis_size("dp") + prior_count * owned_count * lax.axis_size(
        "comp"
    )
    precision = 1.0 / variances
    scaled_means = means * precision
    offset = log_weights - 0.5 * jnp.sum(
        means * scaled_means + jnp.log(variances) + log_two_pi, axis=1
    )

    def rounded(values):
        return lax.reduce_precision(values, exponent_bits=8, mantissa_bits=7)

    def pieces(values):
        first = rounded(values)
        rest = values - first
        second = rounded(rest)
        third = rounded(rest - second)
        return (
            first.astype(jnp.bfloat16),
            second.astype(jnp.bfloat16),
            third.astype(jnp.bfloat16),
        )

    p1, p2, p3 = pieces(-0.5 * precision)
    m1, m2, m3 = pieces(scaled_means)
    loads = jnp.stack([p1.T, p2.T, p3.T, m1.T, m2.T, m3.T])
    exact = descriptors.astype(jnp.float32)
    square = exact * exact
    square_top = rounded(square)
    square_hi = square_top.astype(jnp.bfloat16)
    square_lo = (square - square_top).astype(jnp.bfloat16)
    scores, local_max, local_sum = score_stats(square_hi, square_lo, descriptors, loads, offset)
    local_max = local_max[:, 0]
    local_sum = local_sum[:, 0]
    row_max, row_sum = row_logsumexp_stats(local_max, local_sum, "comp")
    log_total = row_max + jnp.log(row_sum)
    responsibility = jnp.exp(scores - log_total[:, None])
    counts = jnp.sum(responsibility, axis=0)
    resp_half = responsibility.astype(jnp.bfloat16)
    exact_rows = descriptors.astype(jnp.float32)
    halves = jnp.concatenate([descriptors, (exact_rows * exact_rows).astype(jnp.bfloat16)], axis=1)
    moments = lax.dot_general(
        resp_half, halves, (((0,), (0,)), ((), ())), preferred_element_type=jnp.float32
    )
    unit = 8 * (lax.axis_size("dp") // 2)
    padded_rows = -(-(owned_count + 1) // unit) * unit
    packed = jnp.concatenate(
        [
            moments,
            jnp.pad(counts, (0, moments.shape[1] - owned_count))[None, :],
            jnp.zeros((padded_rows - owned_count - 1, moments.shape[1]), jnp.float32),
        ]
    )
    summed = halving_psum(packed, "dp")
    summed_moments = summed[:owned_count]
    summed_counts = summed[owned_count, :owned_count]
    new_log_weights, new_means, new_variances = finish(
        summed_moments, summed_counts, means, variances, grand_total
    )
    return (new_log_weights, new_means, new_variances)


def solution(mesh):
    placed = (P("dp", None), P("comp", None), P("comp", None), P("comp"))
    return jax.shard_map(
        on_device,
        mesh=mesh,
        in_specs=placed,
        out_specs=(P("comp"), P("comp", None), P("comp", None)),
        check_vma=False,
    )
```

```python
import jax
import jax.numpy as jnp
from jax import lax
from jax.experimental import pallas as pl
from jax.sharding import PartitionSpec as P


prior_count = 1.0
log_two_pi = 1.8378770664093453


def finish(moments, counts, means, variances, grand_total):
    feature_width = means.shape[1]
    weight = counts + prior_count
    new_means = (moments[:, :feature_width] + prior_count * means) / weight[:, None]
    new_variances = (
        moments[:, feature_width:] + prior_count * (variances + means * means)
    ) / weight[:, None] - new_means * new_means
    new_log_weights = jnp.log(weight) - jnp.log(grand_total)
    return (new_log_weights, new_means, new_variances)


def score_kernel(hi_ref, lo_ref, x_ref, loads_ref, offset_ref, scores_ref, max_ref, sum_ref):
    def product(piece, features):
        return lax.dot_general(
            loads_ref[piece],
            features,
            (((1,), (1,)), ((), ())),
            preferred_element_type=jnp.float32,
        )

    hi = hi_ref[...]
    lo = lo_ref[...]
    x = x_ref[...]
    total = product(0, hi) + product(0, lo) + product(3, x)
    total = total + (product(1, hi) + product(1, lo) + product(4, x))
    total = total + (product(2, hi) + product(5, x))
    scores = total + offset_ref[...]
    scores_ref[...] = scores
    row_max = jnp.max(scores, axis=0, keepdims=True)
    max_ref[...] = row_max
    sum_ref[...] = jnp.sum(jnp.exp(scores - row_max), axis=0, keepdims=True)


def score_stats(square_hi, square_lo, descriptors, loads, offset):
    rows, width = descriptors.shape
    owned = loads.shape[1]
    block = min(512, rows)
    row_spec = pl.BlockSpec((block, width), lambda i: (i, 0))
    line = jax.ShapeDtypeStruct((1, rows), jnp.float32)
    return pl.pallas_call(
        score_kernel,
        grid=(rows // block,),
        in_specs=[
            row_spec,
            row_spec,
            row_spec,
            pl.BlockSpec(loads.shape, lambda i: (0, 0, 0)),
            pl.BlockSpec((owned, 1), lambda i: (0, 0)),
        ],
        out_specs=[
            pl.BlockSpec((owned, block), lambda i: (0, i)),
            pl.BlockSpec((1, block), lambda i: (0, i)),
            pl.BlockSpec((1, block), lambda i: (0, i)),
        ],
        out_shape=[jax.ShapeDtypeStruct((owned, rows), jnp.float32), line, line],
    )(square_hi, square_lo, descriptors, loads, offset[:, None])


def xor_pairs(size, bit):
    return [(i, i ^ bit) for i in range(size)]


def row_logsumexp_stats(local_max, local_sum, axis):
    size = lax.axis_size(axis)
    row_max, row_sum = local_max, local_sum
    bit = 1
    while bit < size:
        other = lax.ppermute(jnp.stack([row_max, row_sum]), axis, xor_pairs(size, bit))
        other_max, other_sum = other[0], other[1]
        new_max = jnp.maximum(row_max, other_max)
        row_sum = row_sum * jnp.exp(row_max - new_max) + other_sum * jnp.exp(other_max - new_max)
        row_max = new_max
        bit *= 2
    return row_max, row_sum


def halving_psum(rows, axis):
    size = lax.axis_size(axis)
    index = lax.axis_index(axis)
    current = rows
    steps = []
    bit = 1
    while bit < size:
        dim = 1 if bit == 1 else 0
        half = current.shape[dim] // 2
        low = lax.slice_in_dim(current, 0, half, axis=dim)
        high = lax.slice_in_dim(current, half, 2 * half, axis=dim)
        upper = (index // bit) % 2 == 1
        keep = jnp.where(upper, high, low)
        send = jnp.where(upper, low, high)
        current = keep + lax.ppermute(send, axis, xor_pairs(size, bit))
        steps.append((bit, dim))
        bit *= 2
    for bit, dim in reversed(steps):
        upper = (index // bit) % 2 == 1
        other = lax.ppermute(current, axis, xor_pairs(size, bit))
        current = jnp.where(
            upper,
            jnp.concatenate([other, current], axis=dim),
            jnp.concatenate([current, other], axis=dim),
        )
    return current


def on_device(descriptors, means, variances, log_weights):
    row_count = descriptors.shape[0]
    feature_width = descriptors.shape[1]
    owned_count = means.shape[0]
    grand_total = row_count * lax.axis_size("dp") + prior_count * owned_count * lax.axis_size(
        "comp"
    )
    precision = 1.0 / variances
    scaled_means = means * precision
    offset = log_weights - 0.5 * jnp.sum(
        means * scaled_means + jnp.log(variances) + log_two_pi, axis=1
    )

    def rounded(values):
        return lax.reduce_precision(values, exponent_bits=8, mantissa_bits=7)

    def pieces(values):
        first = rounded(values)
        rest = values - first
        second = rounded(rest)
        third = rounded(rest - second)
        return (
            first.astype(jnp.bfloat16),
            second.astype(jnp.bfloat16),
            third.astype(jnp.bfloat16),
        )

    p1, p2, p3 = pieces(-0.5 * precision)
    m1, m2, m3 = pieces(scaled_means)
    loads = jnp.stack([p1, p2, p3, m1, m2, m3])
    exact = descriptors.astype(jnp.float32)
    square = exact * exact
    square_top = rounded(square)
    square_hi = square_top.astype(jnp.bfloat16)
    square_lo = (square - square_top).astype(jnp.bfloat16)
    scores_t, local_max, local_sum = score_stats(square_hi, square_lo, descriptors, loads, offset)
    scores = scores_t.T
    local_max = local_max[0]
    local_sum = local_sum[0]
    row_max, row_sum = row_logsumexp_stats(local_max, local_sum, "comp")
    log_total = row_max + jnp.log(row_sum)
    responsibility = jnp.exp(scores - log_total[:, None])
    counts = jnp.sum(responsibility, axis=0)
    resp_half = responsibility.astype(jnp.bfloat16)
    exact_rows = descriptors.astype(jnp.float32)
    halves = jnp.concatenate([descriptors, (exact_rows * exact_rows).astype(jnp.bfloat16)], axis=1)
    moments = lax.dot_general(
        resp_half, halves, (((0,), (0,)), ((), ())), preferred_element_type=jnp.float32
    )
    unit = 8 * (lax.axis_size("dp") // 2)
    padded_rows = -(-(owned_count + 1) // unit) * unit
    packed = jnp.concatenate(
        [
            moments,
            jnp.pad(counts, (0, moments.shape[1] - owned_count))[None, :],
            jnp.zeros((padded_rows - owned_count - 1, moments.shape[1]), jnp.float32),
        ]
    )
    summed = halving_psum(packed, "dp")
    summed_moments = summed[:owned_count]
    summed_counts = summed[owned_count, :owned_count]
    new_log_weights, new_means, new_variances = finish(
        summed_moments, summed_counts, means, variances, grand_total
    )
    return (new_log_weights, new_means, new_variances)


def solution(mesh):
    placed = (P("dp", None), P("comp", None), P("comp", None), P("comp"))
    return jax.shard_map(
        on_device,
        mesh=mesh,
        in_specs=placed,
        out_specs=(P("comp"), P("comp", None), P("comp", None)),
        check_vma=False,
    )
```

```python
import jax
import jax.numpy as jnp
from jax import lax
from jax.experimental import pallas as pl
from jax.sharding import PartitionSpec as P


prior_count = 1.0
log_two_pi = 1.8378770664093453


def finish(moments, counts, means, variances, grand_total):
    feature_width = means.shape[1]
    weight = counts + prior_count
    new_means = (moments[:, :feature_width] + prior_count * means) / weight[:, None]
    new_variances = (
        moments[:, feature_width:] + prior_count * (variances + means * means)
    ) / weight[:, None] - new_means * new_means
    new_log_weights = jnp.log(weight) - jnp.log(grand_total)
    return (new_log_weights, new_means, new_variances)


def score_kernel(x_ref, load_a_ref, load_b_ref, load_c_ref, offset_ref, scores_ref, max_ref, sum_ref):
    x = x_ref[...]
    exact = x.astype(jnp.float32)
    square = exact * exact
    square_hi = square.astype(jnp.bfloat16)
    square_lo = (square - square_hi.astype(jnp.float32)).astype(jnp.bfloat16)
    wide = jnp.concatenate([square_hi, square_lo, x], axis=1)
    narrow = jnp.concatenate([square_hi, x], axis=1)

    def product(load_ref, features):
        return lax.dot_general(
            load_ref[...],
            features,
            (((1,), (1,)), ((), ())),
            preferred_element_type=jnp.float32,
        )

    total = product(load_a_ref, wide) + product(load_b_ref, wide) + product(load_c_ref, narrow)
    scores = total + offset_ref[...]
    scores_ref[...] = scores
    row_max = jnp.max(scores, axis=0, keepdims=True)
    max_ref[...] = row_max
    sum_ref[...] = jnp.sum(jnp.exp(scores - row_max), axis=0, keepdims=True)


def score_stats(descriptors, load_a, load_b, load_c, offset):
    rows, width = descriptors.shape
    owned = load_a.shape[0]
    block = min(512, rows)
    line = jax.ShapeDtypeStruct((1, rows), jnp.float32)

    def whole(array):
        return pl.BlockSpec(array.shape, lambda i: (0, 0))

    return pl.pallas_call(
        score_kernel,
        grid=(rows // block,),
        in_specs=[
            pl.BlockSpec((block, width), lambda i: (i, 0)),
            whole(load_a),
            whole(load_b),
            whole(load_c),
            pl.BlockSpec((owned, 1), lambda i: (0, 0)),
        ],
        out_specs=[
            pl.BlockSpec((owned, block), lambda i: (0, i)),
            pl.BlockSpec((1, block), lambda i: (0, i)),
            pl.BlockSpec((1, block), lambda i: (0, i)),
        ],
        out_shape=[jax.ShapeDtypeStruct((owned, rows), jnp.float32), line, line],
    )(descriptors, load_a, load_b, load_c, offset[:, None])


def xor_pairs(size, bit):
    return [(i, i ^ bit) for i in range(size)]


def row_logsumexp_stats(local_max, local_sum, axis):
    size = lax.axis_size(axis)
    row_max, row_sum = local_max, local_sum
    bit = 1
    while bit < size:
        other = lax.ppermute(jnp.stack([row_max, row_sum]), axis, xor_pairs(size, bit))
        other_max, other_sum = other[0], other[1]
        new_max = jnp.maximum(row_max, other_max)
        row_sum = row_sum * jnp.exp(row_max - new_max) + other_sum * jnp.exp(other_max - new_max)
        row_max = new_max
        bit *= 2
    return row_max, row_sum


def halving_psum(rows, axis):
    size = lax.axis_size(axis)
    index = lax.axis_index(axis)
    current = rows
    steps = []
    bit = 1
    while bit < size:
        dim = 1 if bit == 1 else 0
        half = current.shape[dim] // 2
        low = lax.slice_in_dim(current, 0, half, axis=dim)
        high = lax.slice_in_dim(current, half, 2 * half, axis=dim)
        upper = (index // bit) % 2 == 1
        keep = jnp.where(upper, high, low)
        send = jnp.where(upper, low, high)
        current = keep + lax.ppermute(send, axis, xor_pairs(size, bit))
        steps.append((bit, dim))
        bit *= 2
    for bit, dim in reversed(steps):
        upper = (index // bit) % 2 == 1
        other = lax.ppermute(current, axis, xor_pairs(size, bit))
        current = jnp.where(
            upper,
            jnp.concatenate([other, current], axis=dim),
            jnp.concatenate([current, other], axis=dim),
        )
    return current


def on_device(descriptors, means, variances, log_weights):
    row_count = descriptors.shape[0]
    feature_width = descriptors.shape[1]
    owned_count = means.shape[0]
    grand_total = row_count * lax.axis_size("dp") + prior_count * owned_count * lax.axis_size(
        "comp"
    )
    precision = 1.0 / variances
    scaled_means = means * precision
    offset = log_weights - 0.5 * jnp.sum(
        means * scaled_means + jnp.log(variances) + log_two_pi, axis=1
    )

    def rounded(values):
        return lax.reduce_precision(values, exponent_bits=8, mantissa_bits=7)

    def pieces(values):
        first = rounded(values)
        rest = values - first
        second = rounded(rest)
        third = rounded(rest - second)
        return (
            first.astype(jnp.bfloat16),
            second.astype(jnp.bfloat16),
            third.astype(jnp.bfloat16),
        )

    p1, p2, p3 = pieces(-0.5 * precision)
    m1, m2, m3 = pieces(scaled_means)
    load_a = jnp.concatenate([p1, p1, m1], axis=1)
    load_b = jnp.concatenate([p2, p2, m2], axis=1)
    load_c = jnp.concatenate([p3, m3], axis=1)
    scores_t, local_max, local_sum = score_stats(descriptors, load_a, load_b, load_c, offset)
    scores = scores_t.T
    local_max = local_max[0]
    local_sum = local_sum[0]
    row_max, row_sum = row_logsumexp_stats(local_max, local_sum, "comp")
    log_total = row_max + jnp.log(row_sum)
    responsibility = jnp.exp(scores - log_total[:, None])
    counts = jnp.sum(responsibility, axis=0)
    resp_half = responsibility.astype(jnp.bfloat16)
    exact_rows = descriptors.astype(jnp.float32)
    halves = jnp.concatenate([descriptors, (exact_rows * exact_rows).astype(jnp.bfloat16)], axis=1)
    moments = lax.dot_general(
        resp_half, halves, (((0,), (0,)), ((), ())), preferred_element_type=jnp.float32
    )
    unit = 8 * (lax.axis_size("dp") // 2)
    padded_rows = -(-(owned_count + 1) // unit) * unit
    packed = jnp.concatenate(
        [
            moments,
            jnp.pad(counts, (0, moments.shape[1] - owned_count))[None, :],
            jnp.zeros((padded_rows - owned_count - 1, moments.shape[1]), jnp.float32),
        ]
    )
    summed = halving_psum(packed, "dp")
    summed_moments = summed[:owned_count]
    summed_counts = summed[owned_count, :owned_count]
    new_log_weights, new_means, new_variances = finish(
        summed_moments, summed_counts, means, variances, grand_total
    )
    return (new_log_weights, new_means, new_variances)


def solution(mesh):
    placed = (P("dp", None), P("comp", None), P("comp", None), P("comp"))
    return jax.shard_map(
        on_device,
        mesh=mesh,
        in_specs=placed,
        out_specs=(P("comp"), P("comp", None), P("comp", None)),
        check_vma=False,
    )
```

```python
import jax
import jax.numpy as jnp
from jax import lax
from jax.experimental import pallas as pl
from jax.sharding import PartitionSpec as P


prior_count = 1.0
log_two_pi = 1.8378770664093453


def finish(moments, counts, means, variances, grand_total):
    feature_width = means.shape[1]
    weight = counts + prior_count
    new_means = (moments[:, :feature_width] + prior_count * means) / weight[:, None]
    new_variances = (
        moments[:, feature_width:] + prior_count * (variances + means * means)
    ) / weight[:, None] - new_means * new_means
    new_log_weights = jnp.log(weight) - jnp.log(grand_total)
    return (new_log_weights, new_means, new_variances)


def score_kernel(x_ref, load_a_ref, load_b_ref, load_c_ref, offset_ref, scores_ref, max_ref, sum_ref):
    x = x_ref[...]
    exact = x.astype(jnp.float32)
    square = exact * exact
    square_hi = square.astype(jnp.bfloat16)
    square_lo = (square - square_hi.astype(jnp.float32)).astype(jnp.bfloat16)
    wide = jnp.concatenate([square_hi, square_lo, x], axis=1)
    narrow = jnp.concatenate([square_hi, x], axis=1)

    def product(load_ref, features):
        return lax.dot_general(
            load_ref[...],
            features,
            (((1,), (1,)), ((), ())),
            preferred_element_type=jnp.float32,
        )

    total = product(load_a_ref, wide) + product(load_b_ref, wide) + product(load_c_ref, narrow)
    scores = total + offset_ref[...]
    scores_ref[...] = scores
    row_max = jnp.max(scores, axis=0, keepdims=True)
    max_ref[...] = row_max
    sum_ref[...] = jnp.sum(jnp.exp(scores - row_max), axis=0, keepdims=True)


def score_stats(descriptors, load_a, load_b, load_c, offset):
    rows, width = descriptors.shape
    owned = load_a.shape[0]
    block = min(1024, rows)
    line = jax.ShapeDtypeStruct((1, rows), jnp.float32)

    def whole(array):
        return pl.BlockSpec(array.shape, lambda i: (0, 0))

    return pl.pallas_call(
        score_kernel,
        grid=(rows // block,),
        in_specs=[
            pl.BlockSpec((block, width), lambda i: (i, 0)),
            whole(load_a),
            whole(load_b),
            whole(load_c),
            pl.BlockSpec((owned, 1), lambda i: (0, 0)),
        ],
        out_specs=[
            pl.BlockSpec((owned, block), lambda i: (0, i)),
            pl.BlockSpec((1, block), lambda i: (0, i)),
            pl.BlockSpec((1, block), lambda i: (0, i)),
        ],
        out_shape=[jax.ShapeDtypeStruct((owned, rows), jnp.float32), line, line],
    )(descriptors, load_a, load_b, load_c, offset[:, None])


def xor_pairs(size, bit):
    return [(i, i ^ bit) for i in range(size)]


def row_logsumexp_stats(local_max, local_sum, axis):
    size = lax.axis_size(axis)
    row_max, row_sum = local_max, local_sum
    bit = 1
    while bit < size:
        other = lax.ppermute(jnp.stack([row_max, row_sum]), axis, xor_pairs(size, bit))
        other_max, other_sum = other[0], other[1]
        new_max = jnp.maximum(row_max, other_max)
        row_sum = row_sum * jnp.exp(row_max - new_max) + other_sum * jnp.exp(other_max - new_max)
        row_max = new_max
        bit *= 2
    return row_max, row_sum


def halving_psum(rows, axis):
    size = lax.axis_size(axis)
    index = lax.axis_index(axis)
    current = rows
    steps = []
    bit = 1
    while bit < size:
        dim = 1 if bit == 1 else 0
        half = current.shape[dim] // 2
        low = lax.slice_in_dim(current, 0, half, axis=dim)
        high = lax.slice_in_dim(current, half, 2 * half, axis=dim)
        upper = (index // bit) % 2 == 1
        keep = jnp.where(upper, high, low)
        send = jnp.where(upper, low, high)
        current = keep + lax.ppermute(send, axis, xor_pairs(size, bit))
        steps.append((bit, dim))
        bit *= 2
    for bit, dim in reversed(steps):
        upper = (index // bit) % 2 == 1
        other = lax.ppermute(current, axis, xor_pairs(size, bit))
        current = jnp.where(
            upper,
            jnp.concatenate([other, current], axis=dim),
            jnp.concatenate([current, other], axis=dim),
        )
    return current


def on_device(descriptors, means, variances, log_weights):
    row_count = descriptors.shape[0]
    feature_width = descriptors.shape[1]
    owned_count = means.shape[0]
    grand_total = row_count * lax.axis_size("dp") + prior_count * owned_count * lax.axis_size(
        "comp"
    )
    precision = 1.0 / variances
    scaled_means = means * precision
    offset = log_weights - 0.5 * jnp.sum(
        means * scaled_means + jnp.log(variances) + log_two_pi, axis=1
    )

    def rounded(values):
        return lax.reduce_precision(values, exponent_bits=8, mantissa_bits=7)

    def pieces(values):
        first = rounded(values)
        rest = values - first
        second = rounded(rest)
        third = rounded(rest - second)
        return (
            first.astype(jnp.bfloat16),
            second.astype(jnp.bfloat16),
            third.astype(jnp.bfloat16),
        )

    p1, p2, p3 = pieces(-0.5 * precision)
    m1, m2, m3 = pieces(scaled_means)
    load_a = jnp.concatenate([p1, p1, m1], axis=1)
    load_b = jnp.concatenate([p2, p2, m2], axis=1)
    load_c = jnp.concatenate([p3, m3], axis=1)
    scores_t, local_max, local_sum = score_stats(descriptors, load_a, load_b, load_c, offset)
    scores = scores_t.T
    local_max = local_max[0]
    local_sum = local_sum[0]
    row_max, row_sum = row_logsumexp_stats(local_max, local_sum, "comp")
    log_total = row_max + jnp.log(row_sum)
    responsibility = jnp.exp(scores - log_total[:, None])
    counts = jnp.sum(responsibility, axis=0)
    resp_half = responsibility.astype(jnp.bfloat16)
    exact_rows = descriptors.astype(jnp.float32)
    halves = jnp.concatenate([descriptors, (exact_rows * exact_rows).astype(jnp.bfloat16)], axis=1)
    moments = lax.dot_general(
        resp_half, halves, (((0,), (0,)), ((), ())), preferred_element_type=jnp.float32
    )
    unit = 8 * (lax.axis_size("dp") // 2)
    padded_rows = -(-(owned_count + 1) // unit) * unit
    packed = jnp.concatenate(
        [
            moments,
            jnp.pad(counts, (0, moments.shape[1] - owned_count))[None, :],
            jnp.zeros((padded_rows - owned_count - 1, moments.shape[1]), jnp.float32),
        ]
    )
    summed = halving_psum(packed, "dp")
    summed_moments = summed[:owned_count]
    summed_counts = summed[owned_count, :owned_count]
    new_log_weights, new_means, new_variances = finish(
        summed_moments, summed_counts, means, variances, grand_total
    )
    return (new_log_weights, new_means, new_variances)


def solution(mesh):
    placed = (P("dp", None), P("comp", None), P("comp", None), P("comp"))
    return jax.shard_map(
        on_device,
        mesh=mesh,
        in_specs=placed,
        out_specs=(P("comp"), P("comp", None), P("comp", None)),
        check_vma=False,
    )
```

```python
import jax
import jax.numpy as jnp
from jax import lax
from jax.experimental import pallas as pl
from jax.sharding import PartitionSpec as P


prior_count = 1.0
log_two_pi = 1.8378770664093453


def finish(moments, counts, means, variances, grand_total):
    feature_width = means.shape[1]
    weight = counts + prior_count
    new_means = (moments[:, :feature_width] + prior_count * means) / weight[:, None]
    new_variances = (
        moments[:, feature_width:] + prior_count * (variances + means * means)
    ) / weight[:, None] - new_means * new_means
    new_log_weights = jnp.log(weight) - jnp.log(grand_total)
    return (new_log_weights, new_means, new_variances)


def score_kernel(x_ref, load_ab_ref, load_c_ref, offset_ref, scores_ref, max_ref, sum_ref):
    x = x_ref[...]
    exact = x.astype(jnp.float32)
    square = exact * exact
    square_hi = square.astype(jnp.bfloat16)
    square_lo = (square - square_hi.astype(jnp.float32)).astype(jnp.bfloat16)
    wide = jnp.concatenate([square_hi, square_lo, x, square_hi, square_lo, x], axis=1)
    narrow = jnp.concatenate([square_hi, x], axis=1)

    def product(load_ref, features):
        return lax.dot_general(
            load_ref[...],
            features,
            (((1,), (1,)), ((), ())),
            preferred_element_type=jnp.float32,
        )

    total = product(load_ab_ref, wide) + product(load_c_ref, narrow)
    scores = total + offset_ref[...]
    scores_ref[...] = scores
    row_max = jnp.max(scores, axis=0, keepdims=True)
    max_ref[...] = row_max
    sum_ref[...] = jnp.sum(jnp.exp(scores - row_max), axis=0, keepdims=True)


def score_stats(descriptors, load_ab, load_c, offset):
    rows, width = descriptors.shape
    owned = load_ab.shape[0]
    block = min(1024, rows)
    line = jax.ShapeDtypeStruct((1, rows), jnp.float32)

    def whole(array):
        return pl.BlockSpec(array.shape, lambda i: (0, 0))

    return pl.pallas_call(
        score_kernel,
        grid=(rows // block,),
        in_specs=[
            pl.BlockSpec((block, width), lambda i: (i, 0)),
            whole(load_ab),
            whole(load_c),
            pl.BlockSpec((owned, 1), lambda i: (0, 0)),
        ],
        out_specs=[
            pl.BlockSpec((owned, block), lambda i: (0, i)),
            pl.BlockSpec((1, block), lambda i: (0, i)),
            pl.BlockSpec((1, block), lambda i: (0, i)),
        ],
        out_shape=[jax.ShapeDtypeStruct((owned, rows), jnp.float32), line, line],
    )(descriptors, load_ab, load_c, offset[:, None])


def xor_pairs(size, bit):
    return [(i, i ^ bit) for i in range(size)]


def row_logsumexp_stats(local_max, local_sum, axis):
    size = lax.axis_size(axis)
    row_max, row_sum = local_max, local_sum
    bit = 1
    while bit < size:
        other = lax.ppermute(jnp.stack([row_max, row_sum]), axis, xor_pairs(size, bit))
        other_max, other_sum = other[0], other[1]
        new_max = jnp.maximum(row_max, other_max)
        row_sum = row_sum * jnp.exp(row_max - new_max) + other_sum * jnp.exp(other_max - new_max)
        row_max = new_max
        bit *= 2
    return row_max, row_sum


def halving_psum(rows, axis):
    size = lax.axis_size(axis)
    index = lax.axis_index(axis)
    current = rows
    steps = []
    bit = 1
    while bit < size:
        dim = 1 if bit == 1 else 0
        half = current.shape[dim] // 2
        low = lax.slice_in_dim(current, 0, half, axis=dim)
        high = lax.slice_in_dim(current, half, 2 * half, axis=dim)
        upper = (index // bit) % 2 == 1
        keep = jnp.where(upper, high, low)
        send = jnp.where(upper, low, high)
        current = keep + lax.ppermute(send, axis, xor_pairs(size, bit))
        steps.append((bit, dim))
        bit *= 2
    for bit, dim in reversed(steps):
        upper = (index // bit) % 2 == 1
        other = lax.ppermute(current, axis, xor_pairs(size, bit))
        current = jnp.where(
            upper,
            jnp.concatenate([other, current], axis=dim),
            jnp.concatenate([current, other], axis=dim),
        )
    return current


def on_device(descriptors, means, variances, log_weights):
    row_count = descriptors.shape[0]
    feature_width = descriptors.shape[1]
    owned_count = means.shape[0]
    grand_total = row_count * lax.axis_size("dp") + prior_count * owned_count * lax.axis_size(
        "comp"
    )
    precision = 1.0 / variances
    scaled_means = means * precision
    offset = log_weights - 0.5 * jnp.sum(
        means * scaled_means + jnp.log(variances) + log_two_pi, axis=1
    )

    def rounded(values):
        return lax.reduce_precision(values, exponent_bits=8, mantissa_bits=7)

    def pieces(values):
        first = rounded(values)
        rest = values - first
        second = rounded(rest)
        third = rounded(rest - second)
        return (
            first.astype(jnp.bfloat16),
            second.astype(jnp.bfloat16),
            third.astype(jnp.bfloat16),
        )

    p1, p2, p3 = pieces(-0.5 * precision)
    m1, m2, m3 = pieces(scaled_means)
    load_ab = jnp.concatenate([p1, p1, m1, p2, p2, m2], axis=1)
    load_c = jnp.concatenate([p3, m3], axis=1)
    scores_t, local_max, local_sum = score_stats(descriptors, load_ab, load_c, offset)
    scores = scores_t.T
    local_max = local_max[0]
    local_sum = local_sum[0]
    row_max, row_sum = row_logsumexp_stats(local_max, local_sum, "comp")
    log_total = row_max + jnp.log(row_sum)
    responsibility = jnp.exp(scores - log_total[:, None])
    counts = jnp.sum(responsibility, axis=0)
    resp_half = responsibility.astype(jnp.bfloat16)
    exact_rows = descriptors.astype(jnp.float32)
    halves = jnp.concatenate([descriptors, (exact_rows * exact_rows).astype(jnp.bfloat16)], axis=1)
    moments = lax.dot_general(
        resp_half, halves, (((0,), (0,)), ((), ())), preferred_element_type=jnp.float32
    )
    unit = 8 * (lax.axis_size("dp") // 2)
    padded_rows = -(-(owned_count + 1) // unit) * unit
    packed = jnp.concatenate(
        [
            moments,
            jnp.pad(counts, (0, moments.shape[1] - owned_count))[None, :],
            jnp.zeros((padded_rows - owned_count - 1, moments.shape[1]), jnp.float32),
        ]
    )
    summed = halving_psum(packed, "dp")
    summed_moments = summed[:owned_count]
    summed_counts = summed[owned_count, :owned_count]
    new_log_weights, new_means, new_variances = finish(
        summed_moments, summed_counts, means, variances, grand_total
    )
    return (new_log_weights, new_means, new_variances)


def solution(mesh):
    placed = (P("dp", None), P("comp", None), P("comp", None), P("comp"))
    return jax.shard_map(
        on_device,
        mesh=mesh,
        in_specs=placed,
        out_specs=(P("comp"), P("comp", None), P("comp", None)),
        check_vma=False,
    )
```

```python
import jax
import jax.numpy as jnp
from jax import lax
from jax.experimental import pallas as pl
from jax.experimental.pallas import tpu as pltpu
from jax.sharding import PartitionSpec as P


prior_count = 1.0
log_two_pi = 1.8378770664093453


def finish(moments, counts, means, variances, grand_total):
    feature_width = means.shape[1]
    weight = counts + prior_count
    new_means = (moments[:, :feature_width] + prior_count * means) / weight[:, None]
    new_variances = (
        moments[:, feature_width:] + prior_count * (variances + means * means)
    ) / weight[:, None] - new_means * new_means
    new_log_weights = jnp.log(weight) - jnp.log(grand_total)
    return (new_log_weights, new_means, new_variances)


def score_kernel(x_ref, load_a_ref, load_b_ref, load_c_ref, offset_ref, scores_ref, max_ref, sum_ref):
    x = x_ref[...]
    exact = x.astype(jnp.float32)
    square = exact * exact
    square_hi = square.astype(jnp.bfloat16)
    square_lo = (square - square_hi.astype(jnp.float32)).astype(jnp.bfloat16)
    wide = jnp.concatenate([square_hi, square_lo, x], axis=1)
    narrow = jnp.concatenate([square_hi, x], axis=1)

    def product(load_ref, features):
        return lax.dot_general(
            load_ref[...],
            features,
            (((1,), (1,)), ((), ())),
            preferred_element_type=jnp.float32,
        )

    total = product(load_a_ref, wide) + product(load_b_ref, wide) + product(load_c_ref, narrow)
    scores = total + offset_ref[...]
    scores_ref[...] = scores
    row_max = jnp.max(scores, axis=0, keepdims=True)
    max_ref[...] = row_max
    sum_ref[...] = jnp.sum(jnp.exp(scores - row_max), axis=0, keepdims=True)


def score_stats(descriptors, load_a, load_b, load_c, offset):
    rows, width = descriptors.shape
    owned = load_a.shape[0]
    block = min(1024, rows)
    line = jax.ShapeDtypeStruct((1, rows), jnp.float32)

    def whole(array):
        return pl.BlockSpec(array.shape, lambda i: (0, 0))

    return pl.pallas_call(
        score_kernel,
        grid=(rows // block,),
        in_specs=[
            pl.BlockSpec((block, width), lambda i: (i, 0)),
            whole(load_a),
            whole(load_b),
            whole(load_c),
            pl.BlockSpec((owned, 1), lambda i: (0, 0)),
        ],
        out_specs=[
            pl.BlockSpec((owned, block), lambda i: (0, i)),
            pl.BlockSpec((1, block), lambda i: (0, i)),
            pl.BlockSpec((1, block), lambda i: (0, i)),
        ],
        out_shape=[jax.ShapeDtypeStruct((owned, rows), jnp.float32), line, line],
    )(descriptors, load_a, load_b, load_c, offset[:, None])


def moment_kernel(scores_ref, total_ref, x_ref, moments_ref, counts_ref):
    @pl.when(pl.program_id(0) == 0)
    def _():
        moments_ref[...] = jnp.zeros_like(moments_ref)
        counts_ref[...] = jnp.zeros_like(counts_ref)

    responsibility = jnp.exp(scores_ref[...] - total_ref[...])
    counts_ref[...] += jnp.sum(responsibility, axis=1, keepdims=True)
    x = x_ref[...]
    exact = x.astype(jnp.float32)
    halves = jnp.concatenate([x, (exact * exact).astype(jnp.bfloat16)], axis=1)
    moments_ref[...] += jnp.dot(
        responsibility.astype(jnp.bfloat16), halves, preferred_element_type=jnp.float32
    )


def moment_sums(scores_t, log_total, descriptors):
    owned, rows = scores_t.shape
    width = descriptors.shape[1]
    block = min(1024, rows)
    return pl.pallas_call(
        moment_kernel,
        grid=(rows // block,),
        in_specs=[
            pl.BlockSpec((owned, block), lambda i: (0, i)),
            pl.BlockSpec((1, block), lambda i: (0, i)),
            pl.BlockSpec((block, width), lambda i: (i, 0)),
        ],
        out_specs=[
            pl.BlockSpec((owned, 2 * width), lambda i: (0, 0)),
            pl.BlockSpec((owned, 1), lambda i: (0, 0)),
        ],
        out_shape=[
            jax.ShapeDtypeStruct((owned, 2 * width), jnp.float32),
            jax.ShapeDtypeStruct((owned, 1), jnp.float32),
        ],
        compiler_params=pltpu.CompilerParams(dimension_semantics=("arbitrary",)),
    )(scores_t, log_total[None, :], descriptors)


def xor_pairs(size, bit):
    return [(i, i ^ bit) for i in range(size)]


def row_logsumexp_stats(local_max, local_sum, axis):
    size = lax.axis_size(axis)
    row_max, row_sum = local_max, local_sum
    bit = 1
    while bit < size:
        other = lax.ppermute(jnp.stack([row_max, row_sum]), axis, xor_pairs(size, bit))
        other_max, other_sum = other[0], other[1]
        new_max = jnp.maximum(row_max, other_max)
        row_sum = row_sum * jnp.exp(row_max - new_max) + other_sum * jnp.exp(other_max - new_max)
        row_max = new_max
        bit *= 2
    return row_max, row_sum


def halving_psum(rows, axis):
    size = lax.axis_size(axis)
    index = lax.axis_index(axis)
    current = rows
    steps = []
    bit = 1
    while bit < size:
        dim = 1 if bit == 1 else 0
        half = current.shape[dim] // 2
        low = lax.slice_in_dim(current, 0, half, axis=dim)
        high = lax.slice_in_dim(current, half, 2 * half, axis=dim)
        upper = (index // bit) % 2 == 1
        keep = jnp.where(upper, high, low)
        send = jnp.where(upper, low, high)
        current = keep + lax.ppermute(send, axis, xor_pairs(size, bit))
        steps.append((bit, dim))
        bit *= 2
    for bit, dim in reversed(steps):
        upper = (index // bit) % 2 == 1
        other = lax.ppermute(current, axis, xor_pairs(size, bit))
        current = jnp.where(
            upper,
            jnp.concatenate([other, current], axis=dim),
            jnp.concatenate([current, other], axis=dim),
        )
    return current


def on_device(descriptors, means, variances, log_weights):
    row_count = descriptors.shape[0]
    feature_width = descriptors.shape[1]
    owned_count = means.shape[0]
    grand_total = row_count * lax.axis_size("dp") + prior_count * owned_count * lax.axis_size(
        "comp"
    )
    precision = 1.0 / variances
    scaled_means = means * precision
    offset = log_weights - 0.5 * jnp.sum(
        means * scaled_means + jnp.log(variances) + log_two_pi, axis=1
    )

    def rounded(values):
        return lax.reduce_precision(values, exponent_bits=8, mantissa_bits=7)

    def pieces(values):
        first = rounded(values)
        rest = values - first
        second = rounded(rest)
        third = rounded(rest - second)
        return (
            first.astype(jnp.bfloat16),
            second.astype(jnp.bfloat16),
            third.astype(jnp.bfloat16),
        )

    p1, p2, p3 = pieces(-0.5 * precision)
    m1, m2, m3 = pieces(scaled_means)
    load_a = jnp.concatenate([p1, p1, m1], axis=1)
    load_b = jnp.concatenate([p2, p2, m2], axis=1)
    load_c = jnp.concatenate([p3, m3], axis=1)
    scores_t, local_max, local_sum = score_stats(descriptors, load_a, load_b, load_c, offset)
    local_max = local_max[0]
    local_sum = local_sum[0]
    row_max, row_sum = row_logsumexp_stats(local_max, local_sum, "comp")
    log_total = row_max + jnp.log(row_sum)
    moments, counts = moment_sums(scores_t, log_total, descriptors)
    counts = counts[:, 0]
    unit = 8 * (lax.axis_size("dp") // 2)
    padded_rows = -(-(owned_count + 1) // unit) * unit
    packed = jnp.concatenate(
        [
            moments,
            jnp.pad(counts, (0, moments.shape[1] - owned_count))[None, :],
            jnp.zeros((padded_rows - owned_count - 1, moments.shape[1]), jnp.float32),
        ]
    )
    summed = halving_psum(packed, "dp")
    summed_moments = summed[:owned_count]
    summed_counts = summed[owned_count, :owned_count]
    new_log_weights, new_means, new_variances = finish(
        summed_moments, summed_counts, means, variances, grand_total
    )
    return (new_log_weights, new_means, new_variances)


def solution(mesh):
    placed = (P("dp", None), P("comp", None), P("comp", None), P("comp"))
    return jax.shard_map(
        on_device,
        mesh=mesh,
        in_specs=placed,
        out_specs=(P("comp"), P("comp", None), P("comp", None)),
        check_vma=False,
    )
```

```python
import jax
import jax.numpy as jnp
from jax import lax
from jax.experimental import pallas as pl
from jax.experimental.pallas import tpu as pltpu
from jax.sharding import PartitionSpec as P


prior_count = 1.0
log_two_pi = 1.8378770664093453


def finish(moments, counts, means, variances, grand_total):
    feature_width = means.shape[1]
    weight = counts + prior_count
    new_means = (moments[:, :feature_width] + prior_count * means) / weight[:, None]
    new_variances = (
        moments[:, feature_width:] + prior_count * (variances + means * means)
    ) / weight[:, None] - new_means * new_means
    new_log_weights = jnp.log(weight) - jnp.log(grand_total)
    return (new_log_weights, new_means, new_variances)


def score_kernel(x_ref, load_a_ref, load_b_ref, load_c_ref, offset_ref, scores_ref, max_ref, sum_ref):
    x = x_ref[...]
    exact = x.astype(jnp.float32)
    square = exact * exact
    square_hi = square.astype(jnp.bfloat16)
    square_lo = (square - square_hi.astype(jnp.float32)).astype(jnp.bfloat16)
    wide = jnp.concatenate([square_hi, square_lo, x], axis=1)
    narrow = jnp.concatenate([square_hi, x], axis=1)

    def product(load_ref, features):
        return lax.dot_general(
            load_ref[...],
            features,
            (((1,), (1,)), ((), ())),
            preferred_element_type=jnp.float32,
        )

    total = product(load_a_ref, wide) + product(load_b_ref, wide) + product(load_c_ref, narrow)
    scores = total + offset_ref[...]
    scores_ref[...] = scores
    row_max = jnp.max(scores, axis=0, keepdims=True)
    max_ref[...] = row_max
    sum_ref[...] = jnp.sum(jnp.exp(scores - row_max), axis=0, keepdims=True)


def score_stats(descriptors, load_a, load_b, load_c, offset):
    rows, width = descriptors.shape
    owned = load_a.shape[0]
    block = min(1024, rows)
    line = jax.ShapeDtypeStruct((1, rows), jnp.float32)

    def whole(array):
        return pl.BlockSpec(array.shape, lambda i: (0, 0))

    return pl.pallas_call(
        score_kernel,
        grid=(rows // block,),
        in_specs=[
            pl.BlockSpec((block, width), lambda i: (i, 0)),
            whole(load_a),
            whole(load_b),
            whole(load_c),
            pl.BlockSpec((owned, 1), lambda i: (0, 0)),
        ],
        out_specs=[
            pl.BlockSpec((owned, block), lambda i: (0, i)),
            pl.BlockSpec((1, block), lambda i: (0, i)),
            pl.BlockSpec((1, block), lambda i: (0, i)),
        ],
        out_shape=[jax.ShapeDtypeStruct((owned, rows), jnp.float32), line, line],
    )(descriptors, load_a, load_b, load_c, offset[:, None])


def moment_kernel(scores_ref, total_ref, x_ref, moments_ref, counts_ref):
    @pl.when(pl.program_id(0) == 0)
    def _():
        moments_ref[...] = jnp.zeros_like(moments_ref)
        counts_ref[...] = jnp.zeros_like(counts_ref)

    responsibility = jnp.exp(scores_ref[...] - total_ref[...])
    counts_ref[...] += jnp.sum(responsibility, axis=1, keepdims=True)
    x = x_ref[...]
    exact = x.astype(jnp.float32)
    halves = jnp.concatenate([x, (exact * exact).astype(jnp.bfloat16)], axis=1)
    moments_ref[...] += jnp.dot(
        responsibility.astype(jnp.bfloat16), halves, preferred_element_type=jnp.float32
    )


def moment_sums(scores_t, log_total, descriptors):
    owned, rows = scores_t.shape
    width = descriptors.shape[1]
    block = min(1024, rows)
    return pl.pallas_call(
        moment_kernel,
        grid=(rows // block,),
        in_specs=[
            pl.BlockSpec((owned, block), lambda i: (0, i)),
            pl.BlockSpec((1, block), lambda i: (0, i)),
            pl.BlockSpec((block, width), lambda i: (i, 0)),
        ],
        out_specs=[
            pl.BlockSpec((owned, 2 * width), lambda i: (0, 0)),
            pl.BlockSpec((owned, 1), lambda i: (0, 0)),
        ],
        out_shape=[
            jax.ShapeDtypeStruct((owned, 2 * width), jnp.float32),
            jax.ShapeDtypeStruct((owned, 1), jnp.float32),
        ],
        compiler_params=pltpu.CompilerParams(dimension_semantics=("arbitrary",)),
    )(scores_t, log_total[None, :], descriptors)


RING_LABELS = {4: (0, 1, 3, 2), 8: (0, 1, 2, 3, 6, 7, 4, 5)}
MESH_INNER = {"dp": 2, "comp": 4}


def position_labels(outer, inner):
    outer_labels = RING_LABELS.get(outer, tuple(range(outer)))
    inner_labels = RING_LABELS.get(inner, tuple(range(inner)))
    return [outer_labels[i // inner] * inner + inner_labels[i % inner] for i in range(outer * inner)]


def xor_pairs(labels, bit):
    position = {label: i for i, label in enumerate(labels)}
    return [(i, position[label ^ bit]) for i, label in enumerate(labels)]


def row_logsumexp_stats(local_max, local_sum, axis, inner):
    size = lax.axis_size(axis)
    labels = position_labels(size // inner, inner)
    row_max, row_sum = local_max, local_sum
    bit = 1
    while bit < size:
        other = lax.ppermute(jnp.stack([row_max, row_sum]), axis, xor_pairs(labels, bit))
        other_max, other_sum = other[0], other[1]
        new_max = jnp.maximum(row_max, other_max)
        row_sum = row_sum * jnp.exp(row_max - new_max) + other_sum * jnp.exp(other_max - new_max)
        row_max = new_max
        bit *= 2
    return row_max, row_sum


def halving_psum(rows, axis, inner):
    size = lax.axis_size(axis)
    labels = position_labels(size // inner, inner)
    index = jnp.array(labels, jnp.int32)[lax.axis_index(axis)]
    current = rows
    steps = []
    bit = 1
    while bit < size:
        dim = 1 if bit == 1 else 0
        half = current.shape[dim] // 2
        low = lax.slice_in_dim(current, 0, half, axis=dim)
        high = lax.slice_in_dim(current, half, 2 * half, axis=dim)
        upper = (index // bit) % 2 == 1
        keep = jnp.where(upper, high, low)
        send = jnp.where(upper, low, high)
        current = keep + lax.ppermute(send, axis, xor_pairs(labels, bit))
        steps.append((bit, dim))
        bit *= 2
    for bit, dim in reversed(steps):
        upper = (index // bit) % 2 == 1
        other = lax.ppermute(current, axis, xor_pairs(labels, bit))
        current = jnp.where(
            upper,
            jnp.concatenate([other, current], axis=dim),
            jnp.concatenate([current, other], axis=dim),
        )
    return current


def on_device(descriptors, means, variances, log_weights):
    row_count = descriptors.shape[0]
    feature_width = descriptors.shape[1]
    owned_count = means.shape[0]
    grand_total = row_count * lax.axis_size("dp") + prior_count * owned_count * lax.axis_size(
        "comp"
    )
    precision = 1.0 / variances
    scaled_means = means * precision
    offset = log_weights - 0.5 * jnp.sum(
        means * scaled_means + jnp.log(variances) + log_two_pi, axis=1
    )

    def rounded(values):
        return lax.reduce_precision(values, exponent_bits=8, mantissa_bits=7)

    def pieces(values):
        first = rounded(values)
        rest = values - first
        second = rounded(rest)
        third = rounded(rest - second)
        return (
            first.astype(jnp.bfloat16),
            second.astype(jnp.bfloat16),
            third.astype(jnp.bfloat16),
        )

    p1, p2, p3 = pieces(-0.5 * precision)
    m1, m2, m3 = pieces(scaled_means)
    load_a = jnp.concatenate([p1, p1, m1], axis=1)
    load_b = jnp.concatenate([p2, p2, m2], axis=1)
    load_c = jnp.concatenate([p3, m3], axis=1)
    scores_t, local_max, local_sum = score_stats(descriptors, load_a, load_b, load_c, offset)
    local_max = local_max[0]
    local_sum = local_sum[0]
    row_max, row_sum = row_logsumexp_stats(local_max, local_sum, "comp", MESH_INNER["comp"])
    log_total = row_max + jnp.log(row_sum)
    moments, counts = moment_sums(scores_t, log_total, descriptors)
    counts = counts[:, 0]
    unit = 8 * (lax.axis_size("dp") // 2)
    padded_rows = -(-(owned_count + 1) // unit) * unit
    packed = jnp.concatenate(
        [
            moments,
            jnp.pad(counts, (0, moments.shape[1] - owned_count))[None, :],
            jnp.zeros((padded_rows - owned_count - 1, moments.shape[1]), jnp.float32),
        ]
    )
    summed = halving_psum(packed, "dp", MESH_INNER["dp"])
    summed_moments = summed[:owned_count]
    summed_counts = summed[owned_count, :owned_count]
    new_log_weights, new_means, new_variances = finish(
        summed_moments, summed_counts, means, variances, grand_total
    )
    return (new_log_weights, new_means, new_variances)


def solution(mesh):
    placed = (P("dp", None), P("comp", None), P("comp", None), P("comp"))
    return jax.shard_map(
        on_device,
        mesh=mesh,
        in_specs=placed,
        out_specs=(P("comp"), P("comp", None), P("comp", None)),
        check_vma=False,
    )
```

```python
import jax
import jax.numpy as jnp
from jax import lax
from jax.experimental import pallas as pl
from jax.experimental.pallas import tpu as pltpu
from jax.sharding import PartitionSpec as P


prior_count = 1.0
log_two_pi = 1.8378770664093453


def finish(moments, counts, means, variances, grand_total):
    feature_width = means.shape[1]
    weight = counts + prior_count
    new_means = (moments[:, :feature_width] + prior_count * means) / weight[:, None]
    new_variances = (
        moments[:, feature_width:] + prior_count * (variances + means * means)
    ) / weight[:, None] - new_means * new_means
    new_log_weights = jnp.log(weight) - jnp.log(grand_total)
    return (new_log_weights, new_means, new_variances)


def score_kernel(
    x_ref, means_ref, variances_ref, weights_ref, scores_ref, max_ref, sum_ref,
    load_a_ref, load_b_ref, load_c_ref, offset_ref,
):
    @pl.when(pl.program_id(0) == 0)
    def _():
        means = means_ref[...]
        variances = variances_ref[...]
        precision = 1.0 / variances
        scaled_means = means * precision

        def pieces(values):
            first = values.astype(jnp.bfloat16)
            rest = values - first.astype(jnp.float32)
            second = rest.astype(jnp.bfloat16)
            third = (rest - second.astype(jnp.float32)).astype(jnp.bfloat16)
            return first, second, third

        p1, p2, p3 = pieces(-0.5 * precision)
        m1, m2, m3 = pieces(scaled_means)
        load_a_ref[...] = jnp.concatenate([p1, p1, m1], axis=1)
        load_b_ref[...] = jnp.concatenate([p2, p2, m2], axis=1)
        load_c_ref[...] = jnp.concatenate([p3, m3], axis=1)
        offset_ref[...] = weights_ref[...] - 0.5 * jnp.sum(
            means * scaled_means + jnp.log(variances) + log_two_pi, axis=1, keepdims=True
        )

    x = x_ref[...]
    exact = x.astype(jnp.float32)
    square = exact * exact
    square_hi = square.astype(jnp.bfloat16)
    square_lo = (square - square_hi.astype(jnp.float32)).astype(jnp.bfloat16)
    wide = jnp.concatenate([square_hi, square_lo, x], axis=1)
    narrow = jnp.concatenate([square_hi, x], axis=1)

    def product(load_ref, features):
        return lax.dot_general(
            load_ref[...],
            features,
            (((1,), (1,)), ((), ())),
            preferred_element_type=jnp.float32,
        )

    total = product(load_a_ref, wide) + product(load_b_ref, wide) + product(load_c_ref, narrow)
    scores = total + offset_ref[...]
    scores_ref[...] = scores
    row_max = jnp.max(scores, axis=0, keepdims=True)
    max_ref[...] = row_max
    sum_ref[...] = jnp.sum(jnp.exp(scores - row_max), axis=0, keepdims=True)


def score_stats(descriptors, means, variances, log_weights):
    rows, width = descriptors.shape
    owned = means.shape[0]
    block = min(1024, rows)
    line = jax.ShapeDtypeStruct((1, rows), jnp.float32)

    def whole(array):
        return pl.BlockSpec(array.shape, lambda i: (0, 0))

    weights = log_weights[:, None]
    return pl.pallas_call(
        score_kernel,
        grid=(rows // block,),
        in_specs=[
            pl.BlockSpec((block, width), lambda i: (i, 0)),
            whole(means),
            whole(variances),
            whole(weights),
        ],
        out_specs=[
            pl.BlockSpec((owned, block), lambda i: (0, i)),
            pl.BlockSpec((1, block), lambda i: (0, i)),
            pl.BlockSpec((1, block), lambda i: (0, i)),
        ],
        out_shape=[jax.ShapeDtypeStruct((owned, rows), jnp.float32), line, line],
        scratch_shapes=[
            pltpu.VMEM((owned, 3 * width), jnp.bfloat16),
            pltpu.VMEM((owned, 3 * width), jnp.bfloat16),
            pltpu.VMEM((owned, 2 * width), jnp.bfloat16),
            pltpu.VMEM((owned, 1), jnp.float32),
        ],
        compiler_params=pltpu.CompilerParams(dimension_semantics=("arbitrary",)),
    )(descriptors, means, variances, weights)


def moment_kernel(scores_ref, total_ref, x_ref, moments_ref, counts_ref):
    @pl.when(pl.program_id(0) == 0)
    def _():
        moments_ref[...] = jnp.zeros_like(moments_ref)
        counts_ref[...] = jnp.zeros_like(counts_ref)

    responsibility = jnp.exp(scores_ref[...] - total_ref[...])
    counts_ref[...] += jnp.sum(responsibility, axis=1, keepdims=True)
    x = x_ref[...]
    exact = x.astype(jnp.float32)
    halves = jnp.concatenate([x, (exact * exact).astype(jnp.bfloat16)], axis=1)
    moments_ref[...] += jnp.dot(
        responsibility.astype(jnp.bfloat16), halves, preferred_element_type=jnp.float32
    )


def moment_sums(scores_t, log_total, descriptors):
    owned, rows = scores_t.shape
    width = descriptors.shape[1]
    block = min(1024, rows)
    return pl.pallas_call(
        moment_kernel,
        grid=(rows // block,),
        in_specs=[
            pl.BlockSpec((owned, block), lambda i: (0, i)),
            pl.BlockSpec((1, block), lambda i: (0, i)),
            pl.BlockSpec((block, width), lambda i: (i, 0)),
        ],
        out_specs=[
            pl.BlockSpec((owned, 2 * width), lambda i: (0, 0)),
            pl.BlockSpec((owned, 1), lambda i: (0, 0)),
        ],
        out_shape=[
            jax.ShapeDtypeStruct((owned, 2 * width), jnp.float32),
            jax.ShapeDtypeStruct((owned, 1), jnp.float32),
        ],
        compiler_params=pltpu.CompilerParams(dimension_semantics=("arbitrary",)),
    )(scores_t, log_total[None, :], descriptors)


RING_LABELS = {4: (0, 1, 3, 2), 8: (0, 1, 2, 3, 6, 7, 4, 5)}
MESH_INNER = {"dp": 2, "comp": 4}


def position_labels(outer, inner):
    outer_labels = RING_LABELS.get(outer, tuple(range(outer)))
    inner_labels = RING_LABELS.get(inner, tuple(range(inner)))
    return [outer_labels[i // inner] * inner + inner_labels[i % inner] for i in range(outer * inner)]


def xor_pairs(labels, bit):
    position = {label: i for i, label in enumerate(labels)}
    return [(i, position[label ^ bit]) for i, label in enumerate(labels)]


def row_logsumexp_stats(local_max, local_sum, axis, inner):
    size = lax.axis_size(axis)
    labels = position_labels(size // inner, inner)
    row_max, row_sum = local_max, local_sum
    bit = 1
    while bit < size:
        other = lax.ppermute(jnp.stack([row_max, row_sum]), axis, xor_pairs(labels, bit))
        other_max, other_sum = other[0], other[1]
        new_max = jnp.maximum(row_max, other_max)
        row_sum = row_sum * jnp.exp(row_max - new_max) + other_sum * jnp.exp(other_max - new_max)
        row_max = new_max
        bit *= 2
    return row_max, row_sum


def halving_psum(rows, axis, inner):
    size = lax.axis_size(axis)
    labels = position_labels(size // inner, inner)
    index = jnp.array(labels, jnp.int32)[lax.axis_index(axis)]
    current = rows
    steps = []
    bit = 1
    while bit < size:
        dim = 1 if bit == 1 else 0
        half = current.shape[dim] // 2
        low = lax.slice_in_dim(current, 0, half, axis=dim)
        high = lax.slice_in_dim(current, half, 2 * half, axis=dim)
        upper = (index // bit) % 2 == 1
        keep = jnp.where(upper, high, low)
        send = jnp.where(upper, low, high)
        current = keep + lax.ppermute(send, axis, xor_pairs(labels, bit))
        steps.append((bit, dim))
        bit *= 2
    for bit, dim in reversed(steps):
        upper = (index // bit) % 2 == 1
        other = lax.ppermute(current, axis, xor_pairs(labels, bit))
        current = jnp.where(
            upper,
            jnp.concatenate([other, current], axis=dim),
            jnp.concatenate([current, other], axis=dim),
        )
    return current


def on_device(descriptors, means, variances, log_weights):
    row_count = descriptors.shape[0]
    feature_width = descriptors.shape[1]
    owned_count = means.shape[0]
    grand_total = row_count * lax.axis_size("dp") + prior_count * owned_count * lax.axis_size(
        "comp"
    )
    scores_t, local_max, local_sum = score_stats(descriptors, means, variances, log_weights)
    local_max = local_max[0]
    local_sum = local_sum[0]
    row_max, row_sum = row_logsumexp_stats(local_max, local_sum, "comp", MESH_INNER["comp"])
    log_total = row_max + jnp.log(row_sum)
    moments, counts = moment_sums(scores_t, log_total, descriptors)
    counts = counts[:, 0]
    unit = 8 * (lax.axis_size("dp") // 2)
    padded_rows = -(-(owned_count + 1) // unit) * unit
    packed = jnp.concatenate(
        [
            moments,
            jnp.pad(counts, (0, moments.shape[1] - owned_count))[None, :],
            jnp.zeros((padded_rows - owned_count - 1, moments.shape[1]), jnp.float32),
        ]
    )
    summed = halving_psum(packed, "dp", MESH_INNER["dp"])
    summed_moments = summed[:owned_count]
    summed_counts = summed[owned_count, :owned_count]
    new_log_weights, new_means, new_variances = finish(
        summed_moments, summed_counts, means, variances, grand_total
    )
    return (new_log_weights, new_means, new_variances)


def solution(mesh):
    placed = (P("dp", None), P("comp", None), P("comp", None), P("comp"))
    return jax.shard_map(
        on_device,
        mesh=mesh,
        in_specs=placed,
        out_specs=(P("comp"), P("comp", None), P("comp", None)),
        check_vma=False,
    )
```

```python
import jax
import jax.numpy as jnp
from jax import lax
from jax.experimental import pallas as pl
from jax.experimental.pallas import tpu as pltpu
from jax.sharding import PartitionSpec as P


prior_count = 1.0
log_two_pi = 1.8378770664093453


def finish(moments, counts, means, variances, grand_total):
    feature_width = means.shape[1]
    weight = counts + prior_count
    new_means = (moments[:, :feature_width] + prior_count * means) / weight[:, None]
    new_variances = (
        moments[:, feature_width:] + prior_count * (variances + means * means)
    ) / weight[:, None] - new_means * new_means
    new_log_weights = jnp.log(weight) - jnp.log(grand_total)
    return (new_log_weights, new_means, new_variances)


def score_kernel(
    x_ref, means_ref, variances_ref, weights_ref, scores_ref, max_ref, sum_ref,
    load_a_ref, load_b_ref, load_c_ref, offset_ref,
):
    @pl.when(pl.program_id(0) == 0)
    def _():
        means = means_ref[...]
        variances = variances_ref[...]
        precision = 1.0 / variances
        scaled_means = means * precision

        def pieces(values):
            first = values.astype(jnp.bfloat16)
            rest = values - first.astype(jnp.float32)
            second = rest.astype(jnp.bfloat16)
            third = (rest - second.astype(jnp.float32)).astype(jnp.bfloat16)
            return first, second, third

        p1, p2, p3 = pieces(-0.5 * precision)
        m1, m2, m3 = pieces(scaled_means)
        load_a_ref[...] = jnp.concatenate([p1, p1, m1], axis=1)
        load_b_ref[...] = jnp.concatenate([p2, p2, m2], axis=1)
        load_c_ref[...] = jnp.concatenate([p3, m3], axis=1)
        offset_ref[...] = weights_ref[...] - 0.5 * jnp.sum(
            means * scaled_means + jnp.log(variances) + log_two_pi, axis=1, keepdims=True
        )

    x = x_ref[...]
    exact = x.astype(jnp.float32)
    square = exact * exact
    square_hi = square.astype(jnp.bfloat16)
    square_lo = (square - square_hi.astype(jnp.float32)).astype(jnp.bfloat16)
    wide = jnp.concatenate([square_hi, square_lo, x], axis=1)
    narrow = jnp.concatenate([square_hi, x], axis=1)

    def product(load_ref, features):
        return lax.dot_general(
            load_ref[...],
            features,
            (((1,), (1,)), ((), ())),
            preferred_element_type=jnp.float32,
        )

    total = product(load_a_ref, wide) + product(load_b_ref, wide) + product(load_c_ref, narrow)
    scores = total + offset_ref[...]
    scores_ref[...] = scores
    row_max = jnp.max(scores, axis=0, keepdims=True)
    max_ref[...] = row_max
    sum_ref[...] = jnp.sum(jnp.exp(scores - row_max), axis=0, keepdims=True)


def score_stats(descriptors, means, variances, log_weights):
    rows, width = descriptors.shape
    owned = means.shape[0]
    block = min(1024, rows)
    line = jax.ShapeDtypeStruct((1, rows), jnp.float32)

    def whole(array):
        return pl.BlockSpec(array.shape, lambda i: (0, 0))

    weights = log_weights[:, None]
    return pl.pallas_call(
        score_kernel,
        grid=(rows // block,),
        in_specs=[
            pl.BlockSpec((block, width), lambda i: (i, 0)),
            whole(means),
            whole(variances),
            whole(weights),
        ],
        out_specs=[
            pl.BlockSpec((owned, block), lambda i: (0, i)),
            pl.BlockSpec((1, block), lambda i: (0, i)),
            pl.BlockSpec((1, block), lambda i: (0, i)),
        ],
        out_shape=[jax.ShapeDtypeStruct((owned, rows), jnp.float32), line, line],
        scratch_shapes=[
            pltpu.VMEM((owned, 3 * width), jnp.bfloat16),
            pltpu.VMEM((owned, 3 * width), jnp.bfloat16),
            pltpu.VMEM((owned, 2 * width), jnp.bfloat16),
            pltpu.VMEM((owned, 1), jnp.float32),
        ],
        compiler_params=pltpu.CompilerParams(dimension_semantics=("arbitrary",)),
    )(descriptors, means, variances, weights)


def moment_kernel(scores_ref, total_ref, x_ref, packed_ref, counts_ref):
    owned = scores_ref.shape[0]

    @pl.when(pl.program_id(0) == 0)
    def _():
        packed_ref[...] = jnp.zeros_like(packed_ref)
        counts_ref[...] = jnp.zeros_like(counts_ref)

    responsibility = jnp.exp(scores_ref[...] - total_ref[...])
    counts_ref[...] += jnp.sum(responsibility, axis=1, keepdims=True)
    x = x_ref[...]
    exact = x.astype(jnp.float32)
    halves = jnp.concatenate([x, (exact * exact).astype(jnp.bfloat16)], axis=1)
    packed_ref[0:owned, :] += jnp.dot(
        responsibility.astype(jnp.bfloat16), halves, preferred_element_type=jnp.float32
    )

    @pl.when(pl.program_id(0) == pl.num_programs(0) - 1)
    def _():
        spread = jnp.broadcast_to(counts_ref[...], (owned, 128))
        packed_ref[owned:owned + 8, :] = jnp.transpose(spread)[0:8, :]


def moment_sums(scores_t, log_total, descriptors, packed_rows):
    owned, rows = scores_t.shape
    width = descriptors.shape[1]
    assert owned == 2 * width
    block = min(1024, rows)
    return pl.pallas_call(
        moment_kernel,
        grid=(rows // block,),
        in_specs=[
            pl.BlockSpec((owned, block), lambda i: (0, i)),
            pl.BlockSpec((1, block), lambda i: (0, i)),
            pl.BlockSpec((block, width), lambda i: (i, 0)),
        ],
        out_specs=pl.BlockSpec((packed_rows, 2 * width), lambda i: (0, 0)),
        out_shape=jax.ShapeDtypeStruct((packed_rows, 2 * width), jnp.float32),
        scratch_shapes=[pltpu.VMEM((owned, 1), jnp.float32)],
        compiler_params=pltpu.CompilerParams(dimension_semantics=("arbitrary",)),
    )(scores_t, log_total[None, :], descriptors)


RING_LABELS = {4: (0, 1, 3, 2), 8: (0, 1, 2, 3, 6, 7, 4, 5)}
MESH_INNER = {"dp": 2, "comp": 4}


def position_labels(outer, inner):
    outer_labels = RING_LABELS.get(outer, tuple(range(outer)))
    inner_labels = RING_LABELS.get(inner, tuple(range(inner)))
    return [outer_labels[i // inner] * inner + inner_labels[i % inner] for i in range(outer * inner)]


def xor_pairs(labels, bit):
    position = {label: i for i, label in enumerate(labels)}
    return [(i, position[label ^ bit]) for i, label in enumerate(labels)]


def row_logsumexp_stats(local_max, local_sum, axis, inner):
    size = lax.axis_size(axis)
    labels = position_labels(size // inner, inner)
    row_max, row_sum = local_max, local_sum
    bit = 1
    while bit < size:
        other = lax.ppermute(jnp.stack([row_max, row_sum]), axis, xor_pairs(labels, bit))
        other_max, other_sum = other[0], other[1]
        new_max = jnp.maximum(row_max, other_max)
        row_sum = row_sum * jnp.exp(row_max - new_max) + other_sum * jnp.exp(other_max - new_max)
        row_max = new_max
        bit *= 2
    return row_max, row_sum


def halving_psum(rows, axis, inner):
    size = lax.axis_size(axis)
    labels = position_labels(size // inner, inner)
    index = jnp.array(labels, jnp.int32)[lax.axis_index(axis)]
    current = rows
    steps = []
    bit = 1
    while bit < size:
        dim = 1 if bit == 1 else 0
        half = current.shape[dim] // 2
        low = lax.slice_in_dim(current, 0, half, axis=dim)
        high = lax.slice_in_dim(current, half, 2 * half, axis=dim)
        upper = (index // bit) % 2 == 1
        keep = jnp.where(upper, high, low)
        send = jnp.where(upper, low, high)
        current = keep + lax.ppermute(send, axis, xor_pairs(labels, bit))
        steps.append((bit, dim))
        bit *= 2
    for bit, dim in reversed(steps):
        upper = (index // bit) % 2 == 1
        other = lax.ppermute(current, axis, xor_pairs(labels, bit))
        current = jnp.where(
            upper,
            jnp.concatenate([other, current], axis=dim),
            jnp.concatenate([current, other], axis=dim),
        )
    return current


def on_device(descriptors, means, variances, log_weights):
    row_count = descriptors.shape[0]
    feature_width = descriptors.shape[1]
    owned_count = means.shape[0]
    grand_total = row_count * lax.axis_size("dp") + prior_count * owned_count * lax.axis_size(
        "comp"
    )
    scores_t, local_max, local_sum = score_stats(descriptors, means, variances, log_weights)
    local_max = local_max[0]
    local_sum = local_sum[0]
    row_max, row_sum = row_logsumexp_stats(local_max, local_sum, "comp", MESH_INNER["comp"])
    log_total = row_max + jnp.log(row_sum)
    unit = 8 * (lax.axis_size("dp") // 2)
    padded_rows = -(-(owned_count + 8) // unit) * unit
    packed = moment_sums(scores_t, log_total, descriptors, padded_rows)
    summed = halving_psum(packed, "dp", MESH_INNER["dp"])
    summed_moments = summed[:owned_count]
    summed_counts = summed[owned_count, :owned_count]
    new_log_weights, new_means, new_variances = finish(
        summed_moments, summed_counts, means, variances, grand_total
    )
    return (new_log_weights, new_means, new_variances)


def solution(mesh):
    placed = (P("dp", None), P("comp", None), P("comp", None), P("comp"))
    return jax.shard_map(
        on_device,
        mesh=mesh,
        in_specs=placed,
        out_specs=(P("comp"), P("comp", None), P("comp", None)),
        check_vma=False,
    )
```

```python
import jax
import jax.numpy as jnp
from jax import lax
from jax.experimental import pallas as pl
from jax.experimental.pallas import tpu as pltpu
from jax.sharding import PartitionSpec as P


prior_count = 1.0
log_two_pi = 1.8378770664093453


def finish(moments, counts, means, variances, grand_total):
    feature_width = means.shape[1]
    weight = counts + prior_count
    new_means = (moments[:, :feature_width] + prior_count * means) / weight[:, None]
    new_variances = (
        moments[:, feature_width:] + prior_count * (variances + means * means)
    ) / weight[:, None] - new_means * new_means
    new_log_weights = jnp.log(weight) - jnp.log(grand_total)
    return (new_log_weights, new_means, new_variances)


def score_kernel(
    x_ref, means_ref, variances_ref, weights_ref, scores_ref, max_ref, sum_ref,
    load_a_ref, load_b_ref, load_c_ref, offset_ref,
):
    @pl.when(pl.program_id(0) == 0)
    def _():
        means = means_ref[...]
        variances = variances_ref[...]
        precision = 1.0 / variances
        scaled_means = means * precision

        def pieces(values):
            first = values.astype(jnp.bfloat16)
            rest = values - first.astype(jnp.float32)
            second = rest.astype(jnp.bfloat16)
            third = (rest - second.astype(jnp.float32)).astype(jnp.bfloat16)
            return first, second, third

        p1, p2, p3 = pieces(-0.5 * precision)
        m1, m2, m3 = pieces(scaled_means)
        load_a_ref[...] = jnp.concatenate([p1, p1, m1], axis=1)
        load_b_ref[...] = jnp.concatenate([p2, p2, m2], axis=1)
        load_c_ref[...] = jnp.concatenate([p3, m3], axis=1)
        weights = jnp.transpose(jnp.broadcast_to(weights_ref[...], (128, means.shape[0])))[:, 0:1]
        offset_ref[...] = weights - 0.5 * jnp.sum(
            means * scaled_means + jnp.log(variances) + log_two_pi, axis=1, keepdims=True
        )

    x = x_ref[...]
    exact = x.astype(jnp.float32)
    square = exact * exact
    square_hi = square.astype(jnp.bfloat16)
    square_lo = (square - square_hi.astype(jnp.float32)).astype(jnp.bfloat16)
    wide = jnp.concatenate([square_hi, square_lo, x], axis=1)
    narrow = jnp.concatenate([square_hi, x], axis=1)

    def product(load_ref, features):
        return lax.dot_general(
            load_ref[...],
            features,
            (((1,), (1,)), ((), ())),
            preferred_element_type=jnp.float32,
        )

    total = product(load_a_ref, wide) + product(load_b_ref, wide) + product(load_c_ref, narrow)
    scores = total + offset_ref[...]
    scores_ref[...] = scores
    row_max = jnp.max(scores, axis=0, keepdims=True)
    max_ref[...] = row_max
    sum_ref[...] = jnp.sum(jnp.exp(scores - row_max), axis=0, keepdims=True)


def score_stats(descriptors, means, variances, log_weights):
    rows, width = descriptors.shape
    owned = means.shape[0]
    block = min(1024, rows)
    line = jax.ShapeDtypeStruct((1, rows), jnp.float32)

    def whole(array):
        return pl.BlockSpec(array.shape, lambda i: (0, 0))

    weights = log_weights[None, :]
    return pl.pallas_call(
        score_kernel,
        grid=(rows // block,),
        in_specs=[
            pl.BlockSpec((block, width), lambda i: (i, 0)),
            whole(means),
            whole(variances),
            whole(weights),
        ],
        out_specs=[
            pl.BlockSpec((owned, block), lambda i: (0, i)),
            pl.BlockSpec((1, block), lambda i: (0, i)),
            pl.BlockSpec((1, block), lambda i: (0, i)),
        ],
        out_shape=[jax.ShapeDtypeStruct((owned, rows), jnp.float32), line, line],
        scratch_shapes=[
            pltpu.VMEM((owned, 3 * width), jnp.bfloat16),
            pltpu.VMEM((owned, 3 * width), jnp.bfloat16),
            pltpu.VMEM((owned, 2 * width), jnp.bfloat16),
            pltpu.VMEM((owned, 1), jnp.float32),
        ],
        compiler_params=pltpu.CompilerParams(dimension_semantics=("arbitrary",)),
    )(descriptors, means, variances, weights)


def moment_kernel(scores_ref, total_ref, x_ref, packed_ref, counts_ref):
    owned = scores_ref.shape[0]

    @pl.when(pl.program_id(0) == 0)
    def _():
        packed_ref[...] = jnp.zeros_like(packed_ref)
        counts_ref[...] = jnp.zeros_like(counts_ref)

    responsibility = jnp.exp(scores_ref[...] - total_ref[...])
    counts_ref[...] += jnp.sum(responsibility, axis=1, keepdims=True)
    x = x_ref[...]
    exact = x.astype(jnp.float32)
    halves = jnp.concatenate([x, (exact * exact).astype(jnp.bfloat16)], axis=1)
    packed_ref[0:owned, :] += jnp.dot(
        responsibility.astype(jnp.bfloat16), halves, preferred_element_type=jnp.float32
    )

    @pl.when(pl.program_id(0) == pl.num_programs(0) - 1)
    def _():
        spread = jnp.broadcast_to(counts_ref[...], (owned, 128))
        packed_ref[owned:owned + 8, :] = jnp.transpose(spread)[0:8, :]


def moment_sums(scores_t, log_total, descriptors, packed_rows):
    owned, rows = scores_t.shape
    width = descriptors.shape[1]
    assert owned == 2 * width
    block = min(1024, rows)
    return pl.pallas_call(
        moment_kernel,
        grid=(rows // block,),
        in_specs=[
            pl.BlockSpec((owned, block), lambda i: (0, i)),
            pl.BlockSpec((1, block), lambda i: (0, i)),
            pl.BlockSpec((block, width), lambda i: (i, 0)),
        ],
        out_specs=pl.BlockSpec((packed_rows, 2 * width), lambda i: (0, 0)),
        out_shape=jax.ShapeDtypeStruct((packed_rows, 2 * width), jnp.float32),
        scratch_shapes=[pltpu.VMEM((owned, 1), jnp.float32)],
        compiler_params=pltpu.CompilerParams(dimension_semantics=("arbitrary",)),
    )(scores_t, log_total[None, :], descriptors)


RING_LABELS = {4: (0, 1, 3, 2), 8: (0, 1, 2, 3, 6, 7, 4, 5)}
MESH_INNER = {"dp": 2, "comp": 4}


def position_labels(outer, inner):
    outer_labels = RING_LABELS.get(outer, tuple(range(outer)))
    inner_labels = RING_LABELS.get(inner, tuple(range(inner)))
    return [outer_labels[i // inner] * inner + inner_labels[i % inner] for i in range(outer * inner)]


def xor_pairs(labels, bit):
    position = {label: i for i, label in enumerate(labels)}
    return [(i, position[label ^ bit]) for i, label in enumerate(labels)]


def row_logsumexp_stats(local_max, local_sum, axis, inner):
    size = lax.axis_size(axis)
    labels = position_labels(size // inner, inner)
    row_max, row_sum = local_max, local_sum
    bit = 1
    while bit < size:
        other = lax.ppermute(jnp.stack([row_max, row_sum]), axis, xor_pairs(labels, bit))
        other_max, other_sum = other[0], other[1]
        new_max = jnp.maximum(row_max, other_max)
        row_sum = row_sum * jnp.exp(row_max - new_max) + other_sum * jnp.exp(other_max - new_max)
        row_max = new_max
        bit *= 2
    return row_max, row_sum


def halving_psum(rows, axis, inner):
    size = lax.axis_size(axis)
    labels = position_labels(size // inner, inner)
    index = jnp.array(labels, jnp.int32)[lax.axis_index(axis)]
    current = rows
    steps = []
    bit = 1
    while bit < size:
        dim = 1 if bit == 1 else 0
        half = current.shape[dim] // 2
        low = lax.slice_in_dim(current, 0, half, axis=dim)
        high = lax.slice_in_dim(current, half, 2 * half, axis=dim)
        upper = (index // bit) % 2 == 1
        keep = jnp.where(upper, high, low)
        send = jnp.where(upper, low, high)
        current = keep + lax.ppermute(send, axis, xor_pairs(labels, bit))
        steps.append((bit, dim))
        bit *= 2
    for bit, dim in reversed(steps):
        upper = (index // bit) % 2 == 1
        other = lax.ppermute(current, axis, xor_pairs(labels, bit))
        current = jnp.where(
            upper,
            jnp.concatenate([other, current], axis=dim),
            jnp.concatenate([current, other], axis=dim),
        )
    return current


def on_device(descriptors, means, variances, log_weights):
    row_count = descriptors.shape[0]
    feature_width = descriptors.shape[1]
    owned_count = means.shape[0]
    grand_total = row_count * lax.axis_size("dp") + prior_count * owned_count * lax.axis_size(
        "comp"
    )
    scores_t, local_max, local_sum = score_stats(descriptors, means, variances, log_weights)
    local_max = local_max[0]
    local_sum = local_sum[0]
    row_max, row_sum = row_logsumexp_stats(local_max, local_sum, "comp", MESH_INNER["comp"])
    log_total = row_max + jnp.log(row_sum)
    unit = 8 * (lax.axis_size("dp") // 2)
    padded_rows = -(-(owned_count + 8) // unit) * unit
    packed = moment_sums(scores_t, log_total, descriptors, padded_rows)
    summed = halving_psum(packed, "dp", MESH_INNER["dp"])
    summed_moments = summed[:owned_count]
    summed_counts = summed[owned_count, :owned_count]
    new_log_weights, new_means, new_variances = finish(
        summed_moments, summed_counts, means, variances, grand_total
    )
    return (new_log_weights, new_means, new_variances)


def solution(mesh):
    placed = (P("dp", None), P("comp", None), P("comp", None), P("comp"))
    return jax.shard_map(
        on_device,
        mesh=mesh,
        in_specs=placed,
        out_specs=(P("comp"), P("comp", None), P("comp", None)),
        check_vma=False,
    )
```

```python
import jax
import jax.numpy as jnp
from jax import lax
from jax.experimental import pallas as pl
from jax.experimental.pallas import tpu as pltpu
from jax.sharding import PartitionSpec as P


prior_count = 1.0
log_two_pi = 1.8378770664093453


def finish(moments, counts, means, variances, grand_total):
    feature_width = means.shape[1]
    weight = counts + prior_count
    new_means = (moments[:, :feature_width] + prior_count * means) / weight[:, None]
    new_variances = (
        moments[:, feature_width:] + prior_count * (variances + means * means)
    ) / weight[:, None] - new_means * new_means
    new_log_weights = jnp.log(weight) - jnp.log(grand_total)
    return (new_log_weights, new_means, new_variances)


def score_kernel(
    x_ref, means_ref, variances_ref, weights_ref, scores_ref, max_ref, sum_ref,
    load_a_ref, load_b_ref, load_c_ref, offset_ref,
):
    @pl.when(pl.program_id(0) == 0)
    def _():
        means = means_ref[...]
        variances = variances_ref[...]
        precision = 1.0 / variances
        scaled_means = means * precision

        def pieces(values):
            first = values.astype(jnp.bfloat16)
            rest = values - first.astype(jnp.float32)
            second = rest.astype(jnp.bfloat16)
            third = (rest - second.astype(jnp.float32)).astype(jnp.bfloat16)
            return first, second, third

        p1, p2, p3 = pieces(-0.5 * precision)
        m1, m2, m3 = pieces(scaled_means)
        load_a_ref[...] = jnp.concatenate([p1, p1, m1], axis=1)
        load_b_ref[...] = jnp.concatenate([p2, p2, m2], axis=1)
        load_c_ref[...] = jnp.concatenate([p3, m3], axis=1)
        weights = jnp.transpose(jnp.broadcast_to(weights_ref[...], (128, means.shape[0])))[:, 0:1]
        offset_ref[...] = weights - 0.5 * jnp.sum(
            means * scaled_means + jnp.log(variances) + log_two_pi, axis=1, keepdims=True
        )

    x = x_ref[...]
    exact = x.astype(jnp.float32)
    square = exact * exact
    square_hi = square.astype(jnp.bfloat16)
    square_lo = (square - square_hi.astype(jnp.float32)).astype(jnp.bfloat16)
    wide = jnp.concatenate([square_hi, square_lo, x], axis=1)
    narrow = jnp.concatenate([square_hi, x], axis=1)

    def product(load_ref, features):
        return lax.dot_general(
            load_ref[...],
            features,
            (((1,), (1,)), ((), ())),
            preferred_element_type=jnp.float32,
        )

    total = product(load_a_ref, wide) + product(load_b_ref, wide) + product(load_c_ref, narrow)
    scores = total + offset_ref[...]
    scores_ref[...] = scores
    row_max = jnp.max(scores, axis=0, keepdims=True)
    max_ref[...] = row_max
    sum_ref[...] = jnp.sum(jnp.exp(scores - row_max), axis=0, keepdims=True)


def score_stats(descriptors, means, variances, log_weights):
    rows, width = descriptors.shape
    owned = means.shape[0]
    block = min(2048, rows)
    line = jax.ShapeDtypeStruct((1, rows), jnp.float32)

    def whole(array):
        return pl.BlockSpec(array.shape, lambda i: (0, 0))

    weights = log_weights[None, :]
    return pl.pallas_call(
        score_kernel,
        grid=(rows // block,),
        in_specs=[
            pl.BlockSpec((block, width), lambda i: (i, 0)),
            whole(means),
            whole(variances),
            whole(weights),
        ],
        out_specs=[
            pl.BlockSpec((owned, block), lambda i: (0, i)),
            pl.BlockSpec((1, block), lambda i: (0, i)),
            pl.BlockSpec((1, block), lambda i: (0, i)),
        ],
        out_shape=[jax.ShapeDtypeStruct((owned, rows), jnp.float32), line, line],
        scratch_shapes=[
            pltpu.VMEM((owned, 3 * width), jnp.bfloat16),
            pltpu.VMEM((owned, 3 * width), jnp.bfloat16),
            pltpu.VMEM((owned, 2 * width), jnp.bfloat16),
            pltpu.VMEM((owned, 1), jnp.float32),
        ],
        compiler_params=pltpu.CompilerParams(dimension_semantics=("arbitrary",)),
    )(descriptors, means, variances, weights)


def moment_kernel(scores_ref, total_ref, x_ref, packed_ref, counts_ref):
    owned = scores_ref.shape[0]

    @pl.when(pl.program_id(0) == 0)
    def _():
        packed_ref[...] = jnp.zeros_like(packed_ref)
        counts_ref[...] = jnp.zeros_like(counts_ref)

    responsibility = jnp.exp(scores_ref[...] - total_ref[...])
    counts_ref[...] += jnp.sum(responsibility, axis=1, keepdims=True)
    x = x_ref[...]
    exact = x.astype(jnp.float32)
    halves = jnp.concatenate([x, (exact * exact).astype(jnp.bfloat16)], axis=1)
    packed_ref[0:owned, :] += jnp.dot(
        responsibility.astype(jnp.bfloat16), halves, preferred_element_type=jnp.float32
    )

    @pl.when(pl.program_id(0) == pl.num_programs(0) - 1)
    def _():
        spread = jnp.broadcast_to(counts_ref[...], (owned, 128))
        packed_ref[owned:owned + 8, :] = jnp.transpose(spread)[0:8, :]


def moment_sums(scores_t, log_total, descriptors, packed_rows):
    owned, rows = scores_t.shape
    width = descriptors.shape[1]
    assert owned == 2 * width
    block = min(2048, rows)
    return pl.pallas_call(
        moment_kernel,
        grid=(rows // block,),
        in_specs=[
            pl.BlockSpec((owned, block), lambda i: (0, i)),
            pl.BlockSpec((1, block), lambda i: (0, i)),
            pl.BlockSpec((block, width), lambda i: (i, 0)),
        ],
        out_specs=pl.BlockSpec((packed_rows, 2 * width), lambda i: (0, 0)),
        out_shape=jax.ShapeDtypeStruct((packed_rows, 2 * width), jnp.float32),
        scratch_shapes=[pltpu.VMEM((owned, 1), jnp.float32)],
        compiler_params=pltpu.CompilerParams(dimension_semantics=("arbitrary",)),
    )(scores_t, log_total[None, :], descriptors)


RING_LABELS = {4: (0, 1, 3, 2), 8: (0, 1, 2, 3, 6, 7, 4, 5)}
MESH_INNER = {"dp": 2, "comp": 4}


def position_labels(outer, inner):
    outer_labels = RING_LABELS.get(outer, tuple(range(outer)))
    inner_labels = RING_LABELS.get(inner, tuple(range(inner)))
    return [outer_labels[i // inner] * inner + inner_labels[i % inner] for i in range(outer * inner)]


def xor_pairs(labels, bit):
    position = {label: i for i, label in enumerate(labels)}
    return [(i, position[label ^ bit]) for i, label in enumerate(labels)]


def row_logsumexp_stats(local_max, local_sum, axis, inner):
    size = lax.axis_size(axis)
    labels = position_labels(size // inner, inner)
    row_max, row_sum = local_max, local_sum
    bit = 1
    while bit < size:
        other = lax.ppermute(jnp.stack([row_max, row_sum]), axis, xor_pairs(labels, bit))
        other_max, other_sum = other[0], other[1]
        new_max = jnp.maximum(row_max, other_max)
        row_sum = row_sum * jnp.exp(row_max - new_max) + other_sum * jnp.exp(other_max - new_max)
        row_max = new_max
        bit *= 2
    return row_max, row_sum


def halving_psum(rows, axis, inner):
    size = lax.axis_size(axis)
    labels = position_labels(size // inner, inner)
    index = jnp.array(labels, jnp.int32)[lax.axis_index(axis)]
    current = rows
    steps = []
    bit = 1
    while bit < size:
        dim = 1 if bit == 1 else 0
        half = current.shape[dim] // 2
        low = lax.slice_in_dim(current, 0, half, axis=dim)
        high = lax.slice_in_dim(current, half, 2 * half, axis=dim)
        upper = (index // bit) % 2 == 1
        keep = jnp.where(upper, high, low)
        send = jnp.where(upper, low, high)
        current = keep + lax.ppermute(send, axis, xor_pairs(labels, bit))
        steps.append((bit, dim))
        bit *= 2
    for bit, dim in reversed(steps):
        upper = (index // bit) % 2 == 1
        other = lax.ppermute(current, axis, xor_pairs(labels, bit))
        current = jnp.where(
            upper,
            jnp.concatenate([other, current], axis=dim),
            jnp.concatenate([current, other], axis=dim),
        )
    return current


def on_device(descriptors, means, variances, log_weights):
    row_count = descriptors.shape[0]
    feature_width = descriptors.shape[1]
    owned_count = means.shape[0]
    grand_total = row_count * lax.axis_size("dp") + prior_count * owned_count * lax.axis_size(
        "comp"
    )
    scores_t, local_max, local_sum = score_stats(descriptors, means, variances, log_weights)
    local_max = local_max[0]
    local_sum = local_sum[0]
    row_max, row_sum = row_logsumexp_stats(local_max, local_sum, "comp", MESH_INNER["comp"])
    log_total = row_max + jnp.log(row_sum)
    unit = 8 * (lax.axis_size("dp") // 2)
    padded_rows = -(-(owned_count + 8) // unit) * unit
    packed = moment_sums(scores_t, log_total, descriptors, padded_rows)
    summed = halving_psum(packed, "dp", MESH_INNER["dp"])
    summed_moments = summed[:owned_count]
    summed_counts = summed[owned_count, :owned_count]
    new_log_weights, new_means, new_variances = finish(
        summed_moments, summed_counts, means, variances, grand_total
    )
    return (new_log_weights, new_means, new_variances)


def solution(mesh):
    placed = (P("dp", None), P("comp", None), P("comp", None), P("comp"))
    return jax.shard_map(
        on_device,
        mesh=mesh,
        in_specs=placed,
        out_specs=(P("comp"), P("comp", None), P("comp", None)),
        check_vma=False,
    )
```
